256 devices in a mesh: blk: 64 (over z, y, x_hi), tp: 4 (over x_lo, core).
Axes of the slice: x: 4 (x_hi: 2, x_lo: 2; x = x_hi * 2 + x_lo), y: 4, z: 8, core: 2. Of those that a mesh axis runs over, the one named last changes fastest.
Arguments:
- q_pre: bfloat16 [16384, 4096], P('blk', 'tp')
- k_pre: bfloat16 [16384, 512], P('blk', 'tp'), may hold values from -4 to 4
- v_pre: bfloat16 [16384, 512], P('blk', 'tp'), may hold values from -6 to 6
- docs: int32 [16384], replicated, may hold values from 0 to 3, never falling along the last dimension, each value on 1 to 10240 neighbouring positions
- q_dec: bfloat16 [12, 4096], P(None, 'tp')
- k_dec: bfloat16 [12, 512], P(None, 'tp'), may hold values from -4 to 4
- v_dec: bfloat16 [12, 512], P(None, 'tp'), may hold values from -6 to 6
- k_cache: bfloat16 [262144, 512], P('blk', 'tp'), may hold values from -4 to 4
- v_cache: bfloat16 [262144, 512], P('blk', 'tp'), may hold values from -6 to 6
- lengths: int32 [12], replicated, may hold values from 2048 to 32768, as said below
- page_map: int32 [2, 2048], P(None, 'blk'), may hold values from 0 to 255, as said below
- w_out: bfloat16 [4096, 4096], P('tp'), may hold values from -0.09375 to 0.09375
- resid_pre: bfloat16 [16384, 4096], P('blk', 'tp'), may hold values from -6 to 6
- resid_dec: bfloat16 [12, 4096], P(None, 'tp'), may hold values from -6 to 6
Outputs:
- out_pre: float32 [16384, 4096], P('blk', 'tp')
- out_dec: float32 [12, 4096], P(None, 'tp')
The draws below stay inside these ranges and needn't reach their ends.
Inputs may be any that keep to these rules, and one draw needn't show every extreme that they name: docs numbers the 4 packed requests in order; every request holds at most 10240 tokens, and one holds exactly that many. `lengths`: one request holds exactly 32768 positions. `page_map`: column g describes cache page g: row 0 is the decode request that owns it, or 12 for a free page; row 1 is its page number within that request (0 on free pages). Request r owns exactly ceil(lengths[r] / 128) pages, numbered from 0, each number once.
All inputs are finite; a program needn't handle non-finite values.
Results may differ from the reference program's by a relative error of at most 0.0028.
Values may be sent and summed in bfloat16 or wider, within the bound.
No kernel may reach another device: no remote copies, remote signals or barrier semaphores. Data moves between devices by JAX's collectives and lax.ppermute only.
A program may use at most 128 MiB of HBM per device.

```python
import math
import jax
import jax.numpy as jnp
import numpy as np
from jax import lax

D = 4096
HEADS = 32
KV_HEADS = 4
HEAD_DIM = 128
PAGE = 128
DEC = 12
PREF_SEQS = 4
TOKENS = 16384
PAGES = 2048
CACHE_LEN = 32768


def spread_heads(source_rows):
    count_rows = source_rows.shape[0]
    group_size = HEADS // KV_HEADS
    shaped = source_rows.reshape(count_rows, KV_HEADS, 1, HEAD_DIM)
    shaped = jnp.broadcast_to(shaped, (count_rows, KV_HEADS, group_size, HEAD_DIM))
    return shaped.reshape(count_rows, HEADS * HEAD_DIM)


def prefill_keys_base(key):
    base_keys = jax.random.normal(jax.random.fold_in(key, 101), (TOKENS, KV_HEADS * HEAD_DIM), jnp.float32)
    base_keys = jnp.clip(base_keys, -4.0, 4.0)
    return base_keys


def draw_k_pre(key, part):
    base_keys = prefill_keys_base(key)
    return base_keys.astype(jnp.bfloat16)


def draw_q_pre(key, part):
    noise_part = jax.random.normal(jax.random.fold_in(key, 104), (TOKENS, HEADS * HEAD_DIM), jnp.float32)
    return (2.5 * jnp.clip(noise_part, -4.5, 4.5)).astype(jnp.bfloat16)


def cache_layout(key):
    shortest = CACHE_LEN // 16
    lengths_drawn = jax.random.randint(jax.random.fold_in(key, 201), (DEC,), shortest, 3 * CACHE_LEN // 8 + 1)
    longest = jax.random.randint(jax.random.fold_in(key, 202), (), 0, DEC)
    lengths_drawn = jnp.where(jnp.arange(DEC) == longest, CACHE_LEN, lengths_drawn).astype(jnp.int32)
    page_needs = (lengths_drawn + PAGE - 1) // PAGE
    page_ends = jnp.cumsum(page_needs).astype(jnp.int32)
    page_starts = page_ends - page_needs
    rotation = jax.random.randint(jax.random.fold_in(key, 203), (), 0, PAGES)
    relative = (jnp.arange(PAGES, dtype=jnp.int32) - rotation) % PAGES
    owners = jnp.sum((relative[:, None] >= page_ends[None, :]).astype(jnp.int32), axis=1).astype(jnp.int32)
    starts_extended = jnp.concatenate([page_starts, page_ends[-1:]])
    within = relative - starts_extended[owners]
    within = jnp.where(owners < DEC, within, 0).astype(jnp.int32)
    first_rows = (page_starts + rotation) % PAGES * PAGE
    return (lengths_drawn, owners, within, first_rows)


def draw_lengths(key, part):
    return cache_layout(key)[0]


def draw_page_map(key, part):
    layout = cache_layout(key)
    return jnp.stack([layout[1], layout[2]]).astype(jnp.int32)


def cache_keys_drawn(key):
    base_cache = jax.random.normal(jax.random.fold_in(key, 204), (PAGES * PAGE, KV_HEADS * HEAD_DIM), jnp.float32)
    base_cache = jnp.clip(base_cache, -4.0, 4.0)
    return base_cache


def draw_k_cache(key, part):
    base_cache = cache_keys_drawn(key)
    return base_cache.astype(jnp.bfloat16)


def own_keys(key):
    drawn = jax.random.normal(jax.random.fold_in(key, 206), (DEC, KV_HEADS * HEAD_DIM), jnp.float32)
    return jnp.clip(drawn, -4.0, 4.0)


def draw_k_dec(key, part):
    return own_keys(key).astype(jnp.bfloat16)


def draw_q_dec(key, part):
    noise_part = jax.random.normal(jax.random.fold_in(key, 207), (DEC, HEADS * HEAD_DIM), jnp.float32)
    return (0.8 * spread_heads(own_keys(key)) + 2.5 * jnp.clip(noise_part, -4.5, 4.5)).astype(jnp.bfloat16)


def levels(rng, dims, shards, low, high):
    level, own = 1.0, jax.random.fold_in(rng, 6)
    for position, parts in shards:
        steps = jnp.exp(jax.random.uniform(jax.random.fold_in(own, position), (parts,), jnp.float32, low / len(shards), high / len(shards)))
        level = level * jnp.repeat(steps, dims[position] // parts).reshape([-1 if axis == position else 1 for axis in range(len(dims))])
    return level


def profile(count, total, most, slope):
    portions = [(1 << 20) // math.isqrt(grade ** slope) + 1 for grade in range(2, count + 1)]
    rest, holding = total - most - (count - 1), [1] * (count - 1)
    while rest > 0:
        free = [i for i in range(count - 1) if holding[i] < most]
        pool, budget = sum([portions[i] for i in free]), rest
        for i in free:
            extra = min(most - holding[i], max(1, budget * portions[i] // pool), rest)
            holding[i] = holding[i] + extra
            rest = rest - extra
    return np.array([most] + holding)


def ragged(rng, number_of, total, limit, slope):
    if number_of == 2:
        one = jax.random.randint(rng, (), max(1, total - limit), min(limit, total - 1) + 1)
        return jnp.stack([one, total - one])
    sizes = jnp.asarray(profile(number_of, total, limit, slope), jnp.int32)
    couples = (number_of - 1) // 2
    source_of, sink = sizes[1:1 + 2 * couples:2], sizes[2:2 + 2 * couples:2]
    margin = jnp.minimum(source_of - 1, limit - sink)
    shifted = jax.random.randint(jax.random.fold_in(rng, 1), (couples,), 0, 1 << 20) % (margin + 1)
    sizes = sizes.at[1:1 + 2 * couples:2].set(source_of - shifted).at[2:2 + 2 * couples:2].set(sink + shifted)
    return sizes[jax.random.permutation(jax.random.fold_in(rng, 2), number_of)]


def scatter_about(rng, extent, scale, reach, split=(), kind=jnp.bfloat16):
    entries = jax.random.normal(rng, extent, jnp.float32) * scale
    if len(split) > 0:
        entries = levels(rng, extent, split, -0.22, 0.18) * entries
    return jnp.clip(entries, min=-reach, max=reach).astype(kind)


def setup_inputs(seed: int = 0) -> dict:
    arg_keys = jax.random.split(jax.random.key(seed), 15)
    return {
        "q_pre": draw_q_pre(jax.random.fold_in(arg_keys[14], 71), 0),
        "k_pre": draw_k_pre(jax.random.fold_in(arg_keys[14], 71), 0),
        "v_pre": scatter_about(arg_keys[2], (TOKENS, KV_HEADS * HEAD_DIM), 1.0, 6.0, ((0, 64), (1, 4))),
        "docs": jnp.searchsorted(jnp.cumsum(ragged(arg_keys[3], PREF_SEQS, TOKENS, 5 * TOKENS // 8, 0)), jnp.arange(TOKENS), side="right").astype(jnp.int32),
        "q_dec": draw_q_dec(jax.random.fold_in(arg_keys[14], 71), 0),
        "k_dec": draw_k_dec(jax.random.fold_in(arg_keys[14], 71), 0),
        "v_dec": scatter_about(arg_keys[6], (DEC, KV_HEADS * HEAD_DIM), 1.0, 6.0, ((1, 4),)),
        "k_cache": draw_k_cache(jax.random.fold_in(arg_keys[14], 71), 0),
        "v_cache": scatter_about(arg_keys[8], (PAGES * PAGE, KV_HEADS * HEAD_DIM), 1.0, 6.0, ((0, 64), (1, 4))),
        "lengths": draw_lengths(jax.random.fold_in(arg_keys[14], 71), 0),
        "page_map": draw_page_map(jax.random.fold_in(arg_keys[14], 71), 0),
        "w_out": scatter_about(arg_keys[11], (HEADS * HEAD_DIM, D), (HEADS * HEAD_DIM) ** -0.5, 0.09375, ((0, 4),)),
        "resid_pre": scatter_about(arg_keys[12], (TOKENS, D), 0.5, 6.0, ((0, 64), (1, 4))),
        "resid_dec": scatter_about(arg_keys[13], (DEC, D), 0.5, 6.0, ((1, 4),)),
    }


NEGATIVE = -1e30


def prefill_attention(q_pre, k_pre, v_pre, docs):
    token_count = q_pre.shape[0]
    query_block = math.gcd(token_count, 128)
    key_window = min(token_count, (5 * token_count) // 8 + query_block)
    group_size = HEADS // KV_HEADS
    factor = HEAD_DIM ** -0.5

    def one_block(block_id):
        query_first = block_id * query_block
        key_first = jnp.clip(query_first + query_block - key_window, 0, token_count - key_window).astype(jnp.int32)
        queries = lax.dynamic_slice_in_dim(q_pre, query_first, query_block, 0).astype(jnp.float32)
        queries = queries.reshape(query_block, KV_HEADS, group_size, HEAD_DIM)
        key_rows = lax.dynamic_slice_in_dim(k_pre, key_first, key_window, 0).astype(jnp.float32)
        key_rows = key_rows.reshape(key_window, KV_HEADS, HEAD_DIM)
        value_rows = lax.dynamic_slice_in_dim(v_pre, key_first, key_window, 0).astype(jnp.float32)
        value_rows = value_rows.reshape(key_window, KV_HEADS, HEAD_DIM)
        query_docs = lax.dynamic_slice_in_dim(docs, query_first, query_block, 0)
        key_docs = lax.dynamic_slice_in_dim(docs, key_first, key_window, 0)
        query_where = query_first + jnp.arange(query_block, dtype=jnp.int32)
        key_where = key_first + jnp.arange(key_window, dtype=jnp.int32)
        visible = (query_docs[:, None] == key_docs[None, :]) & (key_where[None, :] <= query_where[:, None])
        scores = jnp.einsum("qkgd,tkd->kgqt", queries, key_rows) * factor
        scores = jnp.where(visible, scores, NEGATIVE)
        row_top = jnp.max(scores, axis=-1, keepdims=True)
        weights = jnp.where(visible, jnp.exp(scores - row_top), 0.0).astype(jnp.bfloat16)
        weights = lax.optimization_barrier(weights).astype(jnp.float32)
        summed = jnp.einsum("kgqt,tkd->kgqd", weights, value_rows) / jnp.sum(weights, axis=-1)[..., None]
        summed = summed.transpose(2, 0, 1, 3).reshape(query_block, HEADS * HEAD_DIM)
        return summed.astype(jnp.bfloat16)

    blocks = lax.map(one_block, jnp.arange(token_count // query_block, dtype=jnp.int32))
    return blocks.reshape(token_count, HEADS * HEAD_DIM)


def decode_attention(q_dec, k_dec, v_dec, k_cache, v_cache, lengths, page_map):
    cache_rows = k_cache.shape[0]
    group_size = HEADS // KV_HEADS
    factor = HEAD_DIM ** -0.5
    row_owner = jnp.repeat(page_map[0], PAGE)
    row_where = jnp.repeat(page_map[1], PAGE) * PAGE + jnp.tile(jnp.arange(PAGE, dtype=jnp.int32), cache_rows // PAGE)
    key_heads = k_cache.reshape(cache_rows, KV_HEADS, HEAD_DIM)
    value_heads = v_cache.reshape(cache_rows, KV_HEADS, HEAD_DIM)

    def one_request(request):
        live_rows = (row_owner == request) & (row_where < lengths[request])
        query = q_dec[request].reshape(KV_HEADS, group_size, HEAD_DIM)
        own_key = k_dec[request].reshape(KV_HEADS, HEAD_DIM)
        own_value = v_dec[request].reshape(KV_HEADS, HEAD_DIM).astype(jnp.float32)
        results = []
        for head in range(KV_HEADS):
            scores = jnp.dot(key_heads[:, head, :], query[head].T, preferred_element_type=jnp.float32) * factor
            scores = jnp.where(live_rows[:, None], scores, NEGATIVE)
            own_score = jnp.dot(query[head], own_key[head], preferred_element_type=jnp.float32) * factor
            row_top = jnp.maximum(jnp.max(scores, axis=0), own_score)
            weights = jnp.where(live_rows[:, None], jnp.exp(scores - row_top[None, :]), 0.0).astype(jnp.bfloat16)
            weights = lax.optimization_barrier(weights)
            own_weight = jnp.exp(own_score - row_top).astype(jnp.bfloat16)
            own_weight = lax.optimization_barrier(own_weight).astype(jnp.float32)
            numerator = jnp.dot(weights.T, value_heads[:, head, :], preferred_element_type=jnp.float32)
            numerator = numerator + own_weight[:, None] * own_value[head][None, :]
            denominator = jnp.sum(weights.astype(jnp.float32), axis=0) + own_weight
            results.append(numerator / denominator[:, None])
        return jnp.stack(results).reshape(HEADS * HEAD_DIM).astype(jnp.bfloat16)

    return lax.map(one_request, jnp.arange(DEC, dtype=jnp.int32))


def reference(q_pre, k_pre, v_pre, docs, q_dec, k_dec, v_dec, k_cache, v_cache, lengths, page_map, w_out, resid_pre, resid_dec):
    attn_pre = prefill_attention(q_pre, k_pre, v_pre, docs)
    attn_dec = decode_attention(q_dec, k_dec, v_dec, k_cache, v_cache, lengths, page_map)
    out_pre = resid_pre.astype(jnp.float32) + jnp.dot(attn_pre, w_out, preferred_element_type=jnp.float32)
    out_dec = resid_dec.astype(jnp.float32) + jnp.dot(attn_dec, w_out, preferred_element_type=jnp.float32)
    return out_pre, out_dec
```

```python
import jax
import jax.numpy as jnp
from jax import lax
from jax.sharding import Mesh
from jax.sharding import PartitionSpec as P

HEAD_DIM = 128
PAGE = 128
DEC = 12
KEY_BLOCK = 512

NEGATIVE = -1e30

BLK_AXES = ("z", "y", "xh")
TP_AXES = ("xl", "c")


def merge_partials(packed, axis):
    pieces = lax.all_gather(packed, axis, axis=0, tiled=False)
    tops = pieces[..., HEAD_DIM + 1]
    top = jnp.max(tops, axis=0)
    scale = jnp.exp(tops - top[None])
    summed = jnp.sum(pieces[..., : HEAD_DIM + 1] * scale[..., None], axis=0)
    return jnp.concatenate([summed, top[..., None]], axis=-1)


def reduce_scatter_tp(projected):
    rows, width = projected.shape
    quarter = width // 4
    c = lax.axis_index("c")
    xl = lax.axis_index("xl")
    shaped = projected.reshape(rows, 2, 2, quarter)
    keep = lax.dynamic_index_in_dim(shaped, c, axis=2, keepdims=False)
    send = lax.dynamic_index_in_dim(shaped, 1 - c, axis=2, keepdims=False)
    got = lax.ppermute(send, "c", [(0, 1), (1, 0)])
    half = keep + got
    keep = lax.dynamic_index_in_dim(half, xl, axis=1, keepdims=False)
    send = lax.dynamic_index_in_dim(half, 1 - xl, axis=1, keepdims=False)
    got = lax.ppermute(send, "xl", [(0, 1), (1, 0)])
    return keep + got


def on_device(
    q_pre,
    k_pre,
    v_pre,
    docs,
    q_dec,
    k_dec,
    v_dec,
    k_cache,
    v_cache,
    lengths,
    page_map,
    w_out,
    resid_pre,
    resid_dec,
):
    query_rows = q_pre.shape[0]
    local_heads = q_pre.shape[1] // HEAD_DIM
    local_kv = k_pre.shape[1] // HEAD_DIM
    group_size = local_heads // local_kv
    factor = HEAD_DIM ** (-0.5)
    blk_index = (
        lax.axis_index("z") * (lax.axis_size("y") * lax.axis_size("xh"))
        + lax.axis_index("y") * lax.axis_size("xh")
        + lax.axis_index("xh")
    )
    query_start = blk_index * query_rows
    query_docs = lax.dynamic_slice_in_dim(docs, query_start, query_rows, 0)
    query_where = query_start + jnp.arange(query_rows, dtype=jnp.int32)
    grouped = q_pre.reshape(query_rows, local_kv, group_size, HEAD_DIM)

    joined_kv = jnp.concatenate([k_pre, v_pre], axis=1)
    for axis in ("xh", "y", "z"):
        joined_kv = lax.all_gather(joined_kv, axis, axis=0, tiled=True)
    kv_width = k_pre.shape[1]

    doc_start = jnp.sum((docs < query_docs[0]).astype(jnp.int32))
    first_block = doc_start // KEY_BLOCK
    last_block = (query_start + query_rows - 1) // KEY_BLOCK

    def step(block, carried):
        offset = block * KEY_BLOCK
        rows = lax.dynamic_slice_in_dim(joined_kv, offset, KEY_BLOCK, 0)
        key_rows = rows[:, :kv_width]
        value_rows = rows[:, kv_width:]
        key_docs = lax.dynamic_slice_in_dim(docs, offset, KEY_BLOCK, 0)
        key_where = offset + jnp.arange(KEY_BLOCK, dtype=jnp.int32)
        visible = (query_docs[:, None] == key_docs[None, :]) & (
            key_where[None, :] <= query_where[:, None]
        )
        old_top, old_total, old_vector = carried
        scores = (
            jnp.einsum(
                "qkgd,tkd->kgqt",
                grouped,
                key_rows.reshape(KEY_BLOCK, local_kv, HEAD_DIM),
                preferred_element_type=jnp.float32,
            )
            * factor
        )
        scores = jnp.where(visible, scores, NEGATIVE)
        new_top = jnp.maximum(old_top, jnp.max(scores, axis=-1))
        weights = jnp.where(visible, jnp.exp(scores - new_top[..., None]), 0.0).astype(
            jnp.bfloat16
        )
        weights = lax.optimization_barrier(weights)
        rescale = jnp.exp(old_top - new_top)
        new_total = old_total * rescale + jnp.sum(weights.astype(jnp.float32), axis=-1)
        new_vector = old_vector * rescale[..., None] + jnp.einsum(
            "kgqt,tkd->kgqd",
            weights,
            value_rows.reshape(KEY_BLOCK, local_kv, HEAD_DIM),
            preferred_element_type=jnp.float32,
        )
        return (new_top, new_total, new_vector)

    initial = (
        jnp.full((local_kv, group_size, query_rows), NEGATIVE, jnp.float32),
        jnp.zeros((local_kv, group_size, query_rows), jnp.float32),
        jnp.zeros((local_kv, group_size, query_rows, HEAD_DIM), jnp.float32),
    )
    final_top, final_total, final_vector = lax.fori_loop(
        first_block, last_block + 1, step, initial
    )
    attn_pre = (final_vector / final_total[..., None]).transpose(2, 0, 1, 3)
    attn_pre = attn_pre.reshape(query_rows, local_heads * HEAD_DIM).astype(jnp.bfloat16)

    page_count = page_map.shape[1]
    page_owner = page_map[0]
    page_index = page_map[1]
    requests = jnp.arange(DEC, dtype=jnp.int32)
    belongs = page_owner[:, None] == requests[None, :]
    query_pages = jnp.dot(belongs.astype(jnp.bfloat16), q_dec, preferred_element_type=jnp.float32)
    query_pages = query_pages.astype(jnp.bfloat16).reshape(
        page_count, local_kv, group_size, HEAD_DIM
    )
    page_keys = k_cache.reshape(page_count, PAGE, local_kv, HEAD_DIM)
    page_values = v_cache.reshape(page_count, PAGE, local_kv, HEAD_DIM)
    safe_owner = jnp.minimum(page_owner, DEC - 1)
    positions = page_index[:, None] * PAGE + jnp.arange(PAGE, dtype=jnp.int32)[None, :]
    live_rows = (page_owner[:, None] < DEC) & (positions < lengths[safe_owner][:, None])
    live_mask = live_rows[:, None, None, :]
    page_scores = (
        jnp.einsum("pkgd,ptkd->pkgt", query_pages, page_keys, preferred_element_type=jnp.float32)
        * factor
    )
    page_scores = jnp.where(live_mask, page_scores, NEGATIVE)
    page_top = jnp.max(page_scores, axis=-1)
    request_top = jnp.max(jnp.where(belongs[:, :, None, None], page_top[:, None], NEGATIVE), axis=0)
    shared_top = request_top[safe_owner]
    page_weights = jnp.where(live_mask, jnp.exp(page_scores - shared_top[..., None]), 0.0).astype(
        jnp.bfloat16
    )
    page_weights = lax.optimization_barrier(page_weights)
    page_total = jnp.sum(page_weights.astype(jnp.float32), axis=-1)
    page_vector = jnp.einsum(
        "pkgt,ptkd->pkgd", page_weights, page_values, preferred_element_type=jnp.float32
    )
    membership = belongs.astype(jnp.float32)
    request_total = jnp.einsum(
        "pr,pkg->rkg", membership, page_total, precision=lax.Precision.HIGHEST
    )
    request_vector = jnp.einsum(
        "pr,pkgd->rkgd", membership, page_vector, precision=lax.Precision.HIGHEST
    )
    packed = jnp.concatenate(
        [request_vector, request_total[..., None], request_top[..., None]], axis=-1
    )
    for axis in ("xh", "y", "z"):
        packed = merge_partials(packed, axis)
    merged_vector = packed[..., :HEAD_DIM]
    merged_total = packed[..., HEAD_DIM]
    merged_top = packed[..., HEAD_DIM + 1]

    dec_queries = q_dec.reshape(DEC, local_kv, group_size, HEAD_DIM)
    own_scores = (
        jnp.einsum(
            "rkgd,rkd->rkg",
            dec_queries,
            k_dec.reshape(DEC, local_kv, HEAD_DIM),
            preferred_element_type=jnp.float32,
        )
        * factor
    )
    joint_top = jnp.maximum(merged_top, own_scores)
    own_weight = jnp.exp(own_scores - joint_top).astype(jnp.bfloat16)
    own_weight = lax.optimization_barrier(own_weight).astype(jnp.float32)
    carried_scale = jnp.exp(merged_top - joint_top)
    numerator = merged_vector * carried_scale[..., None] + own_weight[..., None] * v_dec.reshape(
        DEC, local_kv, 1, HEAD_DIM
    ).astype(jnp.float32)
    denominator = merged_total * carried_scale + own_weight
    attn_dec = (
        (numerator / denominator[..., None])
        .reshape(DEC, local_heads * HEAD_DIM)
        .astype(jnp.bfloat16)
    )
    joined = jnp.concatenate([attn_pre, attn_dec], axis=0)
    projected = jnp.dot(joined, w_out, preferred_element_type=jnp.float32)
    summed = reduce_scatter_tp(projected)
    out_pre = resid_pre.astype(jnp.float32) + summed[:query_rows]
    out_dec = resid_dec.astype(jnp.float32) + summed[query_rows:]
    return (out_pre, out_dec)


def solution(mesh):
    blk_size, tp_size = mesh.devices.shape
    split_mesh = Mesh(
        mesh.devices.reshape(8, 4, blk_size // 32, 2, tp_size // 2),
        BLK_AXES + TP_AXES,
    )
    blk = BLK_AXES
    tp = TP_AXES
    placed = (
        P(blk, tp),
        P(blk, tp),
        P(blk, tp),
        P(),
        P(None, tp),
        P(None, tp),
        P(None, tp),
        P(blk, tp),
        P(blk, tp),
        P(),
        P(None, blk),
        P(tp, None),
        P(blk, tp),
        P(None, tp),
    )
    return jax.shard_map(
        on_device,
        mesh=split_mesh,
        in_specs=placed,
        out_specs=(P(blk, tp), P(None, tp)),
        check_vma=False,
    )
```

```python
import functools

import jax
import jax.numpy as jnp
from jax import lax
from jax.experimental import pallas as pl
from jax.experimental.pallas import tpu as pltpu
from jax.sharding import Mesh
from jax.sharding import PartitionSpec as P

HEAD_DIM = 128
PAGE = 128
DEC = 12
KEY_BLOCK = 512
LONGEST_DOC = 10240

NEGATIVE = -1e30

BLK_AXES = ("z", "y", "xh")
TP_AXES = ("xl", "c")


def prefill_kernel(first_ref, last_ref, start_ref, q_ref, kv_ref, kdoc_ref, qdoc_ref, o_ref, m_ref, l_ref, acc_ref, *, group, factor):
    step = pl.program_id(0)
    block = first_ref[0] + step

    @pl.when(step == 0)
    def _():
        m_ref[...] = jnp.full(m_ref.shape, NEGATIVE, jnp.float32)
        l_ref[...] = jnp.zeros(l_ref.shape, jnp.float32)
        acc_ref[...] = jnp.zeros(acc_ref.shape, jnp.float32)

    @pl.when(block <= last_ref[0])
    def _():
        kv = kv_ref[...]
        keys = kv[:, :HEAD_DIM]
        values = kv[:, HEAD_DIM:]
        rows = q_ref.shape[0]
        scores = lax.dot_general(
            q_ref[...], keys, (((1,), (1,)), ((), ())), preferred_element_type=jnp.float32
        ) * factor
        query_where = start_ref[0] + lax.broadcasted_iota(jnp.int32, (rows, 1), 0) // group
        key_where = block * KEY_BLOCK + lax.broadcasted_iota(jnp.int32, (1, KEY_BLOCK), 1)
        visible = (qdoc_ref[...] == kdoc_ref[...]) & (key_where <= query_where)
        scores = jnp.where(visible, scores, NEGATIVE)
        old_top = m_ref[...]
        new_top = jnp.maximum(old_top, jnp.max(scores, axis=1, keepdims=True))
        weights = jnp.where(visible, jnp.exp(scores - new_top), 0.0).astype(jnp.bfloat16)
        rescale = jnp.exp(old_top - new_top)
        l_ref[...] = l_ref[...] * rescale + jnp.sum(weights.astype(jnp.float32), axis=1, keepdims=True)
        acc_ref[...] = acc_ref[...] * rescale + jnp.dot(
            weights, values, preferred_element_type=jnp.float32
        )
        m_ref[...] = new_top

    @pl.when(step == pl.num_programs(0) - 1)
    def _():
        o_ref[...] = (acc_ref[...] / l_ref[...]).astype(o_ref.dtype)


def prefill_attention(q_rows, joined_kv, docs, query_docs, query_start, first_block, last_block, group, factor):
    rows = q_rows.shape[0]
    token_count = docs.shape[0]
    steps = min(
        token_count // KEY_BLOCK,
        (LONGEST_DOC - 1 + rows // group - 1) // KEY_BLOCK + 2,
    )
    row_docs = jnp.repeat(query_docs, group)[:, None]
    key_docs = docs.reshape(1, token_count)

    def kv_map(i, first, last, start):
        return (jnp.minimum(first[0] + i, last[0]), 0)

    def doc_map(i, first, last, start):
        return (0, jnp.minimum(first[0] + i, last[0]))

    def fixed(i, first, last, start):
        return (0, 0)

    grid_spec = pltpu.PrefetchScalarGridSpec(
        num_scalar_prefetch=3,
        grid=(steps,),
        in_specs=[
            pl.BlockSpec((rows, HEAD_DIM), fixed),
            pl.BlockSpec((KEY_BLOCK, joined_kv.shape[1]), kv_map),
            pl.BlockSpec((1, KEY_BLOCK), doc_map),
            pl.BlockSpec((rows, 1), fixed),
        ],
        out_specs=pl.BlockSpec((rows, HEAD_DIM), fixed),
        scratch_shapes=[
            pltpu.VMEM((rows, 1), jnp.float32),
            pltpu.VMEM((rows, 1), jnp.float32),
            pltpu.VMEM((rows, HEAD_DIM), jnp.float32),
        ],
    )
    return pl.pallas_call(
        functools.partial(prefill_kernel, group=group, factor=factor),
        grid_spec=grid_spec,
        out_shape=jax.ShapeDtypeStruct((rows, HEAD_DIM), jnp.bfloat16),
        compiler_params=pltpu.CompilerParams(dimension_semantics=("arbitrary",)),
    )(
        jnp.reshape(first_block, (1,)).astype(jnp.int32),
        jnp.reshape(last_block, (1,)).astype(jnp.int32),
        jnp.reshape(query_start, (1,)).astype(jnp.int32),
        q_rows,
        joined_kv,
        key_docs,
        row_docs,
    )


def merge_partials(packed, axis):
    pieces = lax.all_gather(packed, axis, axis=0, tiled=False)
    tops = pieces[..., HEAD_DIM + 1]
    top = jnp.max(tops, axis=0)
    scale = jnp.exp(tops - top[None])
    summed = jnp.sum(pieces[..., : HEAD_DIM + 1] * scale[..., None], axis=0)
    return jnp.concatenate([summed, top[..., None]], axis=-1)


def project_tp(joined, w_out):
    width = w_out.shape[1]
    quarter = width // 4
    c = lax.axis_index("c")
    xl = lax.axis_index("xl")
    shaped_w = w_out.reshape(w_out.shape[0], 2, 2, quarter)
    w_send = lax.dynamic_index_in_dim(shaped_w, 1 - c, axis=2, keepdims=False)
    w_keep = lax.dynamic_index_in_dim(shaped_w, c, axis=2, keepdims=False)
    send = jnp.einsum("rk,kan->ran", joined, w_send, preferred_element_type=jnp.float32)
    got = lax.ppermute(send, "c", [(0, 1), (1, 0)])
    keep = jnp.einsum("rk,kan->ran", joined, w_keep, preferred_element_type=jnp.float32)
    half = keep + got
    keep = lax.dynamic_index_in_dim(half, xl, axis=1, keepdims=False)
    send = lax.dynamic_index_in_dim(half, 1 - xl, axis=1, keepdims=False)
    got = lax.ppermute(send, "xl", [(0, 1), (1, 0)])
    return keep + got


def on_device(
    q_pre,
    k_pre,
    v_pre,
    docs,
    q_dec,
    k_dec,
    v_dec,
    k_cache,
    v_cache,
    lengths,
    page_map,
    w_out,
    resid_pre,
    resid_dec,
):
    query_rows = q_pre.shape[0]
    local_heads = q_pre.shape[1] // HEAD_DIM
    local_kv = k_pre.shape[1] // HEAD_DIM
    group_size = local_heads // local_kv
    factor = HEAD_DIM ** (-0.5)
    blk_index = (
        lax.axis_index("z") * (lax.axis_size("y") * lax.axis_size("xh"))
        + lax.axis_index("y") * lax.axis_size("xh")
        + lax.axis_index("xh")
    )
    query_start = blk_index * query_rows
    query_docs = lax.dynamic_slice_in_dim(docs, query_start, query_rows, 0)

    joined_kv = jnp.concatenate([k_pre, v_pre], axis=1)
    for axis in ("xh", "y", "z"):
        joined_kv = lax.all_gather(joined_kv, axis, axis=0, tiled=True)

    doc_start = jnp.sum((docs < query_docs[0]).astype(jnp.int32))
    first_block = doc_start // KEY_BLOCK
    last_block = (query_start + query_rows - 1) // KEY_BLOCK

    attn_rows = prefill_attention(
        q_pre.reshape(query_rows * local_heads, HEAD_DIM),
        joined_kv,
        docs,
        query_docs,
        query_start,
        first_block,
        last_block,
        group_size,
        factor,
    )
    attn_pre = attn_rows.reshape(query_rows, local_heads * HEAD_DIM)

    page_count = page_map.shape[1]
    page_owner = page_map[0]
    page_index = page_map[1]
    requests = jnp.arange(DEC, dtype=jnp.int32)
    belongs = page_owner[:, None] == requests[None, :]
    query_pages = jnp.dot(belongs.astype(jnp.bfloat16), q_dec, preferred_element_type=jnp.float32)
    query_pages = query_pages.astype(jnp.bfloat16).reshape(
        page_count, local_kv, group_size, HEAD_DIM
    )
    page_keys = k_cache.reshape(page_count, PAGE, local_kv, HEAD_DIM)
    page_values = v_cache.reshape(page_count, PAGE, local_kv, HEAD_DIM)
    safe_owner = jnp.minimum(page_owner, DEC - 1)
    positions = page_index[:, None] * PAGE + jnp.arange(PAGE, dtype=jnp.int32)[None, :]
    live_rows = (page_owner[:, None] < DEC) & (positions < lengths[safe_owner][:, None])
    live_mask = live_rows[:, None, None, :]
    page_scores = (
        jnp.einsum("pkgd,ptkd->pkgt", query_pages, page_keys, preferred_element_type=jnp.float32)
        * factor
    )
    page_scores = jnp.where(live_mask, page_scores, NEGATIVE)
    page_top = jnp.max(page_scores, axis=-1)
    request_top = jnp.max(jnp.where(belongs[:, :, None, None], page_top[:, None], NEGATIVE), axis=0)
    shared_top = request_top[safe_owner]
    page_weights = jnp.where(live_mask, jnp.exp(page_scores - shared_top[..., None]), 0.0).astype(
        jnp.bfloat16
    )
    page_weights = lax.optimization_barrier(page_weights)
    page_total = jnp.sum(page_weights.astype(jnp.float32), axis=-1)
    page_vector = jnp.einsum(
        "pkgt,ptkd->pkgd", page_weights, page_values, preferred_element_type=jnp.float32
    )
    membership = belongs.astype(jnp.float32)
    request_total = jnp.einsum(
        "pr,pkg->rkg", membership, page_total, precision=lax.Precision.HIGHEST
    )
    request_vector = jnp.einsum(
        "pr,pkgd->rkgd", membership, page_vector, precision=lax.Precision.HIGHEST
    )
    packed = jnp.concatenate(
        [request_vector, request_total[..., None], request_top[..., None]], axis=-1
    )
    for axis in ("xh", "y", "z"):
        packed = merge_partials(packed, axis)
    merged_vector = packed[..., :HEAD_DIM]
    merged_total = packed[..., HEAD_DIM]
    merged_top = packed[..., HEAD_DIM + 1]

    dec_queries = q_dec.reshape(DEC, local_kv, group_size, HEAD_DIM)
    own_scores = (
        jnp.einsum(
            "rkgd,rkd->rkg",
            dec_queries,
            k_dec.reshape(DEC, local_kv, HEAD_DIM),
            preferred_element_type=jnp.float32,
        )
        * factor
    )
    joint_top = jnp.maximum(merged_top, own_scores)
    own_weight = jnp.exp(own_scores - joint_top).astype(jnp.bfloat16)
    own_weight = lax.optimization_barrier(own_weight).astype(jnp.float32)
    carried_scale = jnp.exp(merged_top - joint_top)
    numerator = merged_vector * carried_scale[..., None] + own_weight[..., None] * v_dec.reshape(
        DEC, local_kv, 1, HEAD_DIM
    ).astype(jnp.float32)
    denominator = merged_total * carried_scale + own_weight
    attn_dec = (
        (numerator / denominator[..., None])
        .reshape(DEC, local_heads * HEAD_DIM)
        .astype(jnp.bfloat16)
    )
    joined = jnp.concatenate([attn_pre, attn_dec], axis=0)
    summed = project_tp(joined, w_out)
    out_pre = resid_pre.astype(jnp.float32) + summed[:query_rows]
    out_dec = resid_dec.astype(jnp.float32) + summed[query_rows:]
    return (out_pre, out_dec)


def solution(mesh):
    blk_size, tp_size = mesh.devices.shape
    split_mesh = Mesh(
        mesh.devices.reshape(8, 4, blk_size // 32, 2, tp_size // 2),
        BLK_AXES + TP_AXES,
    )
    blk = BLK_AXES
    tp = TP_AXES
    placed = (
        P(blk, tp),
        P(blk, tp),
        P(blk, tp),
        P(),
        P(None, tp),
        P(None, tp),
        P(None, tp),
        P(blk, tp),
        P(blk, tp),
        P(),
        P(None, blk),
        P(tp, None),
        P(blk, tp),
        P(None, tp),
    )
    return jax.shard_map(
        on_device,
        mesh=split_mesh,
        in_specs=placed,
        out_specs=(P(blk, tp), P(None, tp)),
        check_vma=False,
    )
```

```python
import functools

import jax
import jax.numpy as jnp
from jax import lax
from jax.experimental import pallas as pl
from jax.experimental.pallas import tpu as pltpu
from jax.sharding import Mesh
from jax.sharding import PartitionSpec as P

HEAD_DIM = 128
PAGE = 128
DEC = 12
KEY_BLOCK = 512
LONGEST_DOC = 10240

NEGATIVE = -1e30

BLK_AXES = ("z", "y", "xh")
TP_AXES = ("xl", "c")


def prefill_kernel(
    first_ref, last_ref, start_ref, full_ref, q_ref, kv_ref, kdoc_ref, qdoc_ref, o_ref, m_ref, l_ref, acc_ref,
    *, group, factor,
):
    step = pl.program_id(0)
    block = first_ref[0] + step
    active = block <= last_ref[0]
    full = full_ref[jnp.minimum(block, last_ref[0])] == 1

    @pl.when(step == 0)
    def _():
        m_ref[...] = jnp.full(m_ref.shape, NEGATIVE, jnp.float32)
        l_ref[...] = jnp.zeros(l_ref.shape, jnp.float32)
        acc_ref[...] = jnp.zeros(acc_ref.shape, jnp.float32)

    def accumulate(masked):
        kv = kv_ref[...]
        keys = kv[:, :HEAD_DIM]
        values = kv[:, HEAD_DIM:]
        rows = q_ref.shape[0]
        scores = lax.dot_general(
            q_ref[...], keys, (((1,), (1,)), ((), ())), preferred_element_type=jnp.float32
        ) * factor
        old_top = m_ref[...]
        if masked:
            query_where = start_ref[0] + lax.broadcasted_iota(jnp.int32, (rows, 1), 0) // group
            key_where = block * KEY_BLOCK + lax.broadcasted_iota(jnp.int32, (1, KEY_BLOCK), 1)
            visible = (qdoc_ref[...] == kdoc_ref[...]) & (key_where <= query_where)
            scores = jnp.where(visible, scores, NEGATIVE)
            new_top = jnp.maximum(old_top, jnp.max(scores, axis=1, keepdims=True))
            weights = jnp.where(visible, jnp.exp(scores - new_top), 0.0).astype(jnp.bfloat16)
        else:
            new_top = jnp.maximum(old_top, jnp.max(scores, axis=1, keepdims=True))
            weights = jnp.exp(scores - new_top).astype(jnp.bfloat16)
        rescale = jnp.exp(old_top - new_top)
        l_ref[...] = l_ref[...] * rescale + jnp.sum(weights.astype(jnp.float32), axis=1, keepdims=True)
        acc_ref[...] = acc_ref[...] * rescale + jnp.dot(
            weights, values, preferred_element_type=jnp.float32
        )
        m_ref[...] = new_top

    @pl.when(active & full)
    def _():
        accumulate(False)

    @pl.when(active & jnp.logical_not(full))
    def _():
        accumulate(True)

    @pl.when(step == pl.num_programs(0) - 1)
    def _():
        o_ref[...] = (acc_ref[...] / l_ref[...]).astype(o_ref.dtype)


def prefill_attention(q_rows, joined_kv, docs, query_docs, query_start, first_block, last_block, group, factor):
    rows = q_rows.shape[0]
    token_count = docs.shape[0]
    steps = min(
        token_count // KEY_BLOCK,
        (LONGEST_DOC - 1 + rows // group - 1) // KEY_BLOCK + 2,
    )
    row_docs = jnp.repeat(query_docs, group)[:, None]
    block_ids = jnp.arange(token_count // KEY_BLOCK, dtype=jnp.int32)
    full_blocks = (docs[::KEY_BLOCK] == query_docs[-1]) & ((block_ids + 1) * KEY_BLOCK <= query_start)
    key_docs = docs.reshape(1, token_count)

    def kv_map(i, first, last, start, full):
        return (jnp.minimum(first[0] + i, last[0]), 0)

    def doc_map(i, first, last, start, full):
        return (0, jnp.minimum(first[0] + i, last[0]))

    def fixed(i, first, last, start, full):
        return (0, 0)

    grid_spec = pltpu.PrefetchScalarGridSpec(
        num_scalar_prefetch=4,
        grid=(steps,),
        in_specs=[
            pl.BlockSpec((rows, HEAD_DIM), fixed),
            pl.BlockSpec((KEY_BLOCK, joined_kv.shape[1]), kv_map),
            pl.BlockSpec((1, KEY_BLOCK), doc_map),
            pl.BlockSpec((rows, 1), fixed),
        ],
        out_specs=pl.BlockSpec((rows, HEAD_DIM), fixed),
        scratch_shapes=[
            pltpu.VMEM((rows, 1), jnp.float32),
            pltpu.VMEM((rows, 1), jnp.float32),
            pltpu.VMEM((rows, HEAD_DIM), jnp.float32),
        ],
    )
    return pl.pallas_call(
        functools.partial(prefill_kernel, group=group, factor=factor),
        grid_spec=grid_spec,
        out_shape=jax.ShapeDtypeStruct((rows, HEAD_DIM), jnp.bfloat16),
        compiler_params=pltpu.CompilerParams(dimension_semantics=("arbitrary",)),
    )(
        jnp.reshape(first_block, (1,)).astype(jnp.int32),
        jnp.reshape(last_block, (1,)).astype(jnp.int32),
        jnp.reshape(query_start, (1,)).astype(jnp.int32),
        full_blocks.astype(jnp.int32),
        q_rows,
        joined_kv,
        key_docs,
        row_docs,
    )


def merge_partials(packed, axis):
    pieces = lax.all_gather(packed, axis, axis=0, tiled=False)
    tops = pieces[..., HEAD_DIM + 1]
    top = jnp.max(tops, axis=0)
    scale = jnp.exp(tops - top[None])
    summed = jnp.sum(pieces[..., : HEAD_DIM + 1] * scale[..., None], axis=0)
    return jnp.concatenate([summed, top[..., None]], axis=-1)


def project_tp(joined, w_out):
    quarter = w_out.shape[1] // 4
    projected = jnp.dot(joined, w_out, preferred_element_type=jnp.float32)
    parts = [projected[:, j * quarter : (j + 1) * quarter] for j in range(4)]
    first_core = lax.axis_index("c") == 0
    send = jnp.stack(
        [jnp.where(first_core, parts[1], parts[0]), jnp.where(first_core, parts[3], parts[2])], axis=1
    )
    keep = jnp.stack(
        [jnp.where(first_core, parts[0], parts[1]), jnp.where(first_core, parts[2], parts[3])], axis=1
    )
    got = lax.ppermute(send, "c", [(0, 1), (1, 0)])
    half = keep + got
    first_x = lax.axis_index("xl") == 0
    send = jnp.where(first_x, half[:, 1], half[:, 0])
    keep = jnp.where(first_x, half[:, 0], half[:, 1])
    got = lax.ppermute(send, "xl", [(0, 1), (1, 0)])
    return keep + got


def on_device(
    q_pre,
    k_pre,
    v_pre,
    docs,
    q_dec,
    k_dec,
    v_dec,
    k_cache,
    v_cache,
    lengths,
    page_map,
    w_out,
    resid_pre,
    resid_dec,
):
    query_rows = q_pre.shape[0]
    local_heads = q_pre.shape[1] // HEAD_DIM
    local_kv = k_pre.shape[1] // HEAD_DIM
    group_size = local_heads // local_kv
    factor = HEAD_DIM ** (-0.5)
    blk_index = (
        lax.axis_index("z") * (lax.axis_size("y") * lax.axis_size("xh"))
        + lax.axis_index("y") * lax.axis_size("xh")
        + lax.axis_index("xh")
    )
    query_start = blk_index * query_rows
    query_docs = lax.dynamic_slice_in_dim(docs, query_start, query_rows, 0)

    joined_kv = jnp.concatenate([k_pre, v_pre], axis=1)
    for axis in ("xh", "y", "z"):
        joined_kv = lax.all_gather(joined_kv, axis, axis=0, tiled=True)

    doc_start = jnp.sum((docs < query_docs[0]).astype(jnp.int32))
    first_block = doc_start // KEY_BLOCK
    last_block = (query_start + query_rows - 1) // KEY_BLOCK

    attn_rows = prefill_attention(
        q_pre.reshape(query_rows * local_heads, HEAD_DIM),
        joined_kv,
        docs,
        query_docs,
        query_start,
        first_block,
        last_block,
        group_size,
        factor,
    )
    attn_pre = attn_rows.reshape(query_rows, local_heads * HEAD_DIM)

    page_count = page_map.shape[1]
    page_owner = page_map[0]
    page_index = page_map[1]
    requests = jnp.arange(DEC, dtype=jnp.int32)
    belongs = page_owner[:, None] == requests[None, :]
    query_pages = jnp.dot(belongs.astype(jnp.bfloat16), q_dec, preferred_element_type=jnp.float32)
    query_pages = query_pages.astype(jnp.bfloat16).reshape(
        page_count, local_kv, group_size, HEAD_DIM
    )
    page_keys = k_cache.reshape(page_count, PAGE, local_kv, HEAD_DIM)
    page_values = v_cache.reshape(page_count, PAGE, local_kv, HEAD_DIM)
    safe_owner = jnp.minimum(page_owner, DEC - 1)
    positions = page_index[:, None] * PAGE + jnp.arange(PAGE, dtype=jnp.int32)[None, :]
    live_rows = (page_owner[:, None] < DEC) & (positions < lengths[safe_owner][:, None])
    live_mask = live_rows[:, None, None, :]
    page_scores = (
        jnp.einsum("pkgd,ptkd->pkgt", query_pages, page_keys, preferred_element_type=jnp.float32)
        * factor
    )
    page_scores = jnp.where(live_mask, page_scores, NEGATIVE)
    page_top = jnp.max(page_scores, axis=-1)
    request_top = jnp.max(jnp.where(belongs[:, :, None, None], page_top[:, None], NEGATIVE), axis=0)
    shared_top = request_top[safe_owner]
    page_weights = jnp.where(live_mask, jnp.exp(page_scores - shared_top[..., None]), 0.0).astype(
        jnp.bfloat16
    )
    page_weights = lax.optimization_barrier(page_weights)
    page_total = jnp.sum(page_weights.astype(jnp.float32), axis=-1)
    page_vector = jnp.einsum(
        "pkgt,ptkd->pkgd", page_weights, page_values, preferred_element_type=jnp.float32
    )
    membership = belongs.astype(jnp.float32)
    request_total = jnp.einsum(
        "pr,pkg->rkg", membership, page_total, precision=lax.Precision.HIGHEST
    )
    request_vector = jnp.einsum(
        "pr,pkgd->rkgd", membership, page_vector, precision=lax.Precision.HIGHEST
    )
    packed = jnp.concatenate(
        [request_vector, request_total[..., None], request_top[..., None]], axis=-1
    )
    packed = merge_partials(packed, BLK_AXES)
    merged_vector = packed[..., :HEAD_DIM]
    merged_total = packed[..., HEAD_DIM]
    merged_top = packed[..., HEAD_DIM + 1]

    dec_queries = q_dec.reshape(DEC, local_kv, group_size, HEAD_DIM)
    own_scores = (
        jnp.einsum(
            "rkgd,rkd->rkg",
            dec_queries,
            k_dec.reshape(DEC, local_kv, HEAD_DIM),
            preferred_element_type=jnp.float32,
        )
        * factor
    )
    joint_top = jnp.maximum(merged_top, own_scores)
    own_weight = jnp.exp(own_scores - joint_top).astype(jnp.bfloat16)
    own_weight = lax.optimization_barrier(own_weight).astype(jnp.float32)
    carried_scale = jnp.exp(merged_top - joint_top)
    numerator = merged_vector * carried_scale[..., None] + own_weight[..., None] * v_dec.reshape(
        DEC, local_kv, 1, HEAD_DIM
    ).astype(jnp.float32)
    denominator = merged_total * carried_scale + own_weight
    attn_dec = (
        (numerator / denominator[..., None])
        .reshape(DEC, local_heads * HEAD_DIM)
        .astype(jnp.bfloat16)
    )
    joined = jnp.concatenate([attn_pre, attn_dec], axis=0)
    summed = project_tp(joined, w_out)
    out_pre = resid_pre.astype(jnp.float32) + summed[:query_rows]
    out_dec = resid_dec.astype(jnp.float32) + summed[query_rows:]
    return (out_pre, out_dec)


def solution(mesh):
    blk_size, tp_size = mesh.devices.shape
    split_mesh = Mesh(
        mesh.devices.reshape(8, 4, blk_size // 32, 2, tp_size // 2),
        BLK_AXES + TP_AXES,
    )
    blk = BLK_AXES
    tp = TP_AXES
    placed = (
        P(blk, tp),
        P(blk, tp),
        P(blk, tp),
        P(),
        P(None, tp),
        P(None, tp),
        P(None, tp),
        P(blk, tp),
        P(blk, tp),
        P(),
        P(None, blk),
        P(tp, None),
        P(blk, tp),
        P(None, tp),
    )
    return jax.shard_map(
        on_device,
        mesh=split_mesh,
        in_specs=placed,
        out_specs=(P(blk, tp), P(None, tp)),
        check_vma=False,
    )
```

```python
import functools

import jax
import jax.numpy as jnp
from jax import lax
from jax.experimental import pallas as pl
from jax.experimental.pallas import tpu as pltpu
from jax.sharding import Mesh
from jax.sharding import PartitionSpec as P

HEAD_DIM = 128
PAGE = 128
DEC = 12
KEY_BLOCK = 512
LONGEST_DOC = 10240

NEGATIVE = -1e30

BLK_AXES = ("z", "y", "xh")
TP_AXES = ("xl", "c")


def prefill_kernel(
    first_ref, last_ref, start_ref, full_ref, q_ref, kv_ref, kdoc_ref, qdoc_ref, o_ref, m_ref, l_ref, acc_ref,
    *, group, factor,
):
    step = pl.program_id(0)
    block = first_ref[0] + step
    active = block <= last_ref[0]
    full = full_ref[jnp.minimum(block, last_ref[0])] == 1

    @pl.when(step == 0)
    def _():
        m_ref[...] = jnp.full(m_ref.shape, NEGATIVE, jnp.float32)
        l_ref[...] = jnp.zeros(l_ref.shape, jnp.float32)
        acc_ref[...] = jnp.zeros(acc_ref.shape, jnp.float32)

    def accumulate(masked):
        kv = kv_ref[...]
        keys = kv[:, :HEAD_DIM]
        values = kv[:, HEAD_DIM:]
        rows = q_ref.shape[0]
        scores = lax.dot_general(
            q_ref[...], keys, (((1,), (1,)), ((), ())), preferred_element_type=jnp.float32
        ) * factor
        old_top = m_ref[...]
        if masked:
            query_where = start_ref[0] + lax.broadcasted_iota(jnp.int32, (rows, 1), 0) // group
            key_where = block * KEY_BLOCK + lax.broadcasted_iota(jnp.int32, (1, KEY_BLOCK), 1)
            visible = (qdoc_ref[...] == kdoc_ref[...]) & (key_where <= query_where)
            scores = jnp.where(visible, scores, NEGATIVE)
            new_top = jnp.maximum(old_top, jnp.max(scores, axis=1, keepdims=True))
            weights = jnp.where(visible, jnp.exp(scores - new_top), 0.0).astype(jnp.bfloat16)
        else:
            new_top = jnp.maximum(old_top, jnp.max(scores, axis=1, keepdims=True))
            weights = jnp.exp(scores - new_top).astype(jnp.bfloat16)
        rescale = jnp.exp(old_top - new_top)
        l_ref[...] = l_ref[...] * rescale + jnp.sum(weights.astype(jnp.float32), axis=1, keepdims=True)
        acc_ref[...] = acc_ref[...] * rescale + jnp.dot(
            weights, values, preferred_element_type=jnp.float32
        )
        m_ref[...] = new_top

    @pl.when(active & full)
    def _():
        accumulate(False)

    @pl.when(active & jnp.logical_not(full))
    def _():
        accumulate(True)

    @pl.when(step == pl.num_programs(0) - 1)
    def _():
        o_ref[...] = (acc_ref[...] / l_ref[...]).astype(o_ref.dtype)


def prefill_attention(q_rows, joined_kv, docs, query_docs, query_start, first_block, last_block, group, factor):
    rows = q_rows.shape[0]
    token_count = docs.shape[0]
    steps = min(
        token_count // KEY_BLOCK,
        (LONGEST_DOC - 1 + rows // group - 1) // KEY_BLOCK + 2,
    )
    row_docs = jnp.repeat(query_docs, group)[:, None]
    block_ids = jnp.arange(token_count // KEY_BLOCK, dtype=jnp.int32)
    full_blocks = (docs[::KEY_BLOCK] == query_docs[-1]) & ((block_ids + 1) * KEY_BLOCK <= query_start)
    key_docs = docs.reshape(1, token_count)

    def kv_map(i, first, last, start, full):
        return (jnp.minimum(first[0] + i, last[0]), 0)

    def doc_map(i, first, last, start, full):
        return (0, jnp.minimum(first[0] + i, last[0]))

    def fixed(i, first, last, start, full):
        return (0, 0)

    grid_spec = pltpu.PrefetchScalarGridSpec(
        num_scalar_prefetch=4,
        grid=(steps,),
        in_specs=[
            pl.BlockSpec((rows, HEAD_DIM), fixed),
            pl.BlockSpec((KEY_BLOCK, joined_kv.shape[1]), kv_map),
            pl.BlockSpec((1, KEY_BLOCK), doc_map),
            pl.BlockSpec((rows, 1), fixed),
        ],
        out_specs=pl.BlockSpec((rows, HEAD_DIM), fixed),
        scratch_shapes=[
            pltpu.VMEM((rows, 1), jnp.float32),
            pltpu.VMEM((rows, 1), jnp.float32),
            pltpu.VMEM((rows, HEAD_DIM), jnp.float32),
        ],
    )
    return pl.pallas_call(
        functools.partial(prefill_kernel, group=group, factor=factor),
        grid_spec=grid_spec,
        out_shape=jax.ShapeDtypeStruct((rows, HEAD_DIM), jnp.bfloat16),
        compiler_params=pltpu.CompilerParams(dimension_semantics=("arbitrary",)),
    )(
        jnp.reshape(first_block, (1,)).astype(jnp.int32),
        jnp.reshape(last_block, (1,)).astype(jnp.int32),
        jnp.reshape(query_start, (1,)).astype(jnp.int32),
        full_blocks.astype(jnp.int32),
        q_rows,
        joined_kv,
        key_docs,
        row_docs,
    )


def merge_partials(packed, axis):
    pieces = lax.all_gather(packed, axis, axis=0, tiled=False)
    tops = pieces[..., HEAD_DIM + 1]
    top = jnp.max(tops, axis=0)
    scale = jnp.exp(tops - top[None])
    summed = jnp.sum(pieces[..., : HEAD_DIM + 1] * scale[..., None], axis=0)
    return jnp.concatenate([summed, top[..., None]], axis=-1)


def project_tp(joined, w_out):
    quarter = w_out.shape[1] // 4
    projected = jnp.dot(joined, w_out, preferred_element_type=jnp.float32)
    parts = [projected[:, j * quarter : (j + 1) * quarter] for j in range(4)]
    first_core = lax.axis_index("c") == 0
    send = jnp.stack(
        [jnp.where(first_core, parts[1], parts[0]), jnp.where(first_core, parts[3], parts[2])], axis=1
    )
    keep = jnp.stack(
        [jnp.where(first_core, parts[0], parts[1]), jnp.where(first_core, parts[2], parts[3])], axis=1
    )
    got = lax.ppermute(send, "c", [(0, 1), (1, 0)])
    half = keep + got
    first_x = lax.axis_index("xl") == 0
    send = jnp.where(first_x, half[:, 1], half[:, 0])
    keep = jnp.where(first_x, half[:, 0], half[:, 1])
    got = lax.ppermute(send, "xl", [(0, 1), (1, 0)])
    return keep + got


def on_device(
    q_pre,
    k_pre,
    v_pre,
    docs,
    q_dec,
    k_dec,
    v_dec,
    k_cache,
    v_cache,
    lengths,
    page_map,
    w_out,
    resid_pre,
    resid_dec,
):
    query_rows = q_pre.shape[0]
    local_heads = q_pre.shape[1] // HEAD_DIM
    local_kv = k_pre.shape[1] // HEAD_DIM
    group_size = local_heads // local_kv
    factor = HEAD_DIM ** (-0.5)
    blk_index = (
        lax.axis_index("z") * (lax.axis_size("y") * lax.axis_size("xh"))
        + lax.axis_index("y") * lax.axis_size("xh")
        + lax.axis_index("xh")
    )
    query_start = blk_index * query_rows
    query_docs = lax.dynamic_slice_in_dim(docs, query_start, query_rows, 0)

    joined_kv = jnp.concatenate([k_pre, v_pre], axis=1)
    for axis in ("xh", "y", "z"):
        joined_kv = lax.all_gather(joined_kv, axis, axis=0, tiled=True)

    doc_start = jnp.sum((docs < query_docs[0]).astype(jnp.int32))
    first_block = doc_start // KEY_BLOCK
    last_block = (query_start + query_rows - 1) // KEY_BLOCK

    attn_rows = prefill_attention(
        q_pre.reshape(query_rows * local_heads, HEAD_DIM),
        joined_kv,
        docs,
        query_docs,
        query_start,
        first_block,
        last_block,
        group_size,
        factor,
    )
    attn_pre = attn_rows.reshape(query_rows, local_heads * HEAD_DIM)

    page_count = page_map.shape[1]
    page_owner = page_map[0]
    page_index = page_map[1]
    requests = jnp.arange(DEC, dtype=jnp.int32)
    belongs = page_owner[:, None] == requests[None, :]
    query_pages = jnp.dot(belongs.astype(jnp.bfloat16), q_dec, preferred_element_type=jnp.float32)
    query_pages = query_pages.astype(jnp.bfloat16).reshape(
        page_count, local_kv, group_size, HEAD_DIM
    )
    page_keys = k_cache.reshape(page_count, PAGE, local_kv, HEAD_DIM)
    page_values = v_cache.reshape(page_count, PAGE, local_kv, HEAD_DIM)
    safe_owner = jnp.minimum(page_owner, DEC - 1)
    positions = page_index[:, None] * PAGE + jnp.arange(PAGE, dtype=jnp.int32)[None, :]
    live_rows = (page_owner[:, None] < DEC) & (positions < lengths[safe_owner][:, None])
    live_mask = live_rows[:, None, None, :]
    page_scores = (
        jnp.einsum("pkgd,ptkd->pkgt", query_pages, page_keys, preferred_element_type=jnp.float32)
        * factor
    )
    page_scores = jnp.where(live_mask, page_scores, NEGATIVE)
    page_top = jnp.max(page_scores, axis=-1)
    request_top = jnp.max(jnp.where(belongs[:, :, None, None], page_top[:, None], NEGATIVE), axis=0)
    shared_top = request_top[safe_owner]
    page_weights = jnp.where(live_mask, jnp.exp(page_scores - shared_top[..., None]), 0.0).astype(
        jnp.bfloat16
    )
    page_weights = lax.optimization_barrier(page_weights)
    page_total = jnp.sum(page_weights.astype(jnp.float32), axis=-1)
    page_vector = jnp.einsum(
        "pkgt,ptkd->pkgd", page_weights, page_values, preferred_element_type=jnp.float32
    )
    membership = belongs.astype(jnp.float32)
    request_total = jnp.einsum(
        "pr,pkg->rkg", membership, page_total, precision=lax.Precision.HIGHEST
    )
    request_vector = jnp.einsum(
        "pr,pkgd->rkgd", membership, page_vector, precision=lax.Precision.HIGHEST
    )
    packed = jnp.concatenate(
        [request_vector, request_total[..., None], request_top[..., None]], axis=-1
    )
    for axis in ("xh", "y", "z"):
        packed = merge_partials(packed, axis)
    merged_vector = packed[..., :HEAD_DIM]
    merged_total = packed[..., HEAD_DIM]
    merged_top = packed[..., HEAD_DIM + 1]

    dec_queries = q_dec.reshape(DEC, local_kv, group_size, HEAD_DIM)
    own_scores = (
        jnp.einsum(
            "rkgd,rkd->rkg",
            dec_queries,
            k_dec.reshape(DEC, local_kv, HEAD_DIM),
            preferred_element_type=jnp.float32,
        )
        * factor
    )
    joint_top = jnp.maximum(merged_top, own_scores)
    own_weight = jnp.exp(own_scores - joint_top).astype(jnp.bfloat16)
    own_weight = lax.optimization_barrier(own_weight).astype(jnp.float32)
    carried_scale = jnp.exp(merged_top - joint_top)
    numerator = merged_vector * carried_scale[..., None] + own_weight[..., None] * v_dec.reshape(
        DEC, local_kv, 1, HEAD_DIM
    ).astype(jnp.float32)
    denominator = merged_total * carried_scale + own_weight
    attn_dec = (
        (numerator / denominator[..., None])
        .reshape(DEC, local_heads * HEAD_DIM)
        .astype(jnp.bfloat16)
    )
    joined = jnp.concatenate([attn_pre, attn_dec], axis=0)
    summed = project_tp(joined, w_out)
    out_pre = resid_pre.astype(jnp.float32) + summed[:query_rows]
    out_dec = resid_dec.astype(jnp.float32) + summed[query_rows:]
    return (out_pre, out_dec)


def solution(mesh):
    blk_size, tp_size = mesh.devices.shape
    split_mesh = Mesh(
        mesh.devices.reshape(8, 4, blk_size // 32, 2, tp_size // 2),
        BLK_AXES + TP_AXES,
    )
    blk = BLK_AXES
    tp = TP_AXES
    placed = (
        P(blk, tp),
        P(blk, tp),
        P(blk, tp),
        P(),
        P(None, tp),
        P(None, tp),
        P(None, tp),
        P(blk, tp),
        P(blk, tp),
        P(),
        P(None, blk),
        P(tp, None),
        P(blk, tp),
        P(None, tp),
    )
    return jax.shard_map(
        on_device,
        mesh=split_mesh,
        in_specs=placed,
        out_specs=(P(blk, tp), P(None, tp)),
        check_vma=False,
    )
```

```python
import functools

import jax
import jax.numpy as jnp
from jax import lax
from jax.experimental import pallas as pl
from jax.experimental.pallas import tpu as pltpu
from jax.sharding import Mesh
from jax.sharding import PartitionSpec as P

HEAD_DIM = 128
PAGE = 128
DEC = 12
KEY_BLOCK = 512
LONGEST_DOC = 10240

NEGATIVE = -1e30

BLK_AXES = ("z", "y", "xh")
TP_AXES = ("xl", "c")


def prefill_kernel(
    first_ref, last_ref, start_ref, kind_ref, bdoc_ref, q_ref, kv_ref, kdoc_ref, qdoc_ref, o_ref, m_ref, l_ref,
    acc_ref, *, group, factor,
):
    step = pl.program_id(0)
    block = first_ref[0] + step
    active = block <= last_ref[0]
    clamped = jnp.minimum(block, last_ref[0])
    kind = kind_ref[clamped]

    @pl.when(step == 0)
    def _():
        m_ref[...] = jnp.full(m_ref.shape, NEGATIVE, jnp.float32)
        l_ref[...] = jnp.zeros(l_ref.shape, jnp.float32)
        acc_ref[...] = jnp.zeros(acc_ref.shape, jnp.float32)

    def accumulate(mode):
        kv = kv_ref[...]
        keys = kv[:, :HEAD_DIM]
        values = kv[:, HEAD_DIM:]
        rows = q_ref.shape[0]
        scores = lax.dot_general(
            q_ref[...], keys, (((1,), (1,)), ((), ())), preferred_element_type=jnp.float32
        ) * factor
        old_top = m_ref[...]
        if mode == 0:
            query_where = start_ref[0] + lax.broadcasted_iota(jnp.int32, (rows, 1), 0) // group
            key_where = block * KEY_BLOCK + lax.broadcasted_iota(jnp.int32, (1, KEY_BLOCK), 1)
            visible = (qdoc_ref[...] == kdoc_ref[...]) & (key_where <= query_where)
            scores = jnp.where(visible, scores, NEGATIVE)
            new_top = jnp.maximum(old_top, jnp.max(scores, axis=1, keepdims=True))
            weights = jnp.where(visible, jnp.exp(scores - new_top), 0.0).astype(jnp.bfloat16)
        else:
            new_top = jnp.maximum(old_top, jnp.max(scores, axis=1, keepdims=True))
            weights = jnp.exp(scores - new_top).astype(jnp.bfloat16)
        rescale = jnp.exp(old_top - new_top)
        new_total = l_ref[...] * rescale + jnp.sum(weights.astype(jnp.float32), axis=1, keepdims=True)
        new_vector = acc_ref[...] * rescale + jnp.dot(
            weights, values, preferred_element_type=jnp.float32
        )
        if mode == 2:
            seen = qdoc_ref[...] == bdoc_ref[clamped]
            new_top = jnp.where(seen, new_top, old_top)
            new_total = jnp.where(seen, new_total, l_ref[...])
            new_vector = jnp.where(seen, new_vector, acc_ref[...])
        l_ref[...] = new_total
        acc_ref[...] = new_vector
        m_ref[...] = new_top

    for mode in (0, 1, 2):

        @pl.when(active & (kind == mode))
        def _():
            accumulate(mode)

    @pl.when(step == pl.num_programs(0) - 1)
    def _():
        o_ref[...] = (acc_ref[...] / l_ref[...]).astype(o_ref.dtype)


def prefill_attention(q_rows, joined_kv, docs, query_docs, query_start, first_block, last_block, group, factor):
    rows = q_rows.shape[0]
    token_count = docs.shape[0]
    steps = min(
        token_count // KEY_BLOCK,
        (LONGEST_DOC - 1 + rows // group - 1) // KEY_BLOCK + 2,
    )
    row_docs = jnp.repeat(query_docs, group)[:, None]
    block_ids = jnp.arange(token_count // KEY_BLOCK, dtype=jnp.int32)
    block_docs = docs[::KEY_BLOCK]
    one_doc = (block_docs == docs[KEY_BLOCK - 1 :: KEY_BLOCK]) & (
        (block_ids + 1) * KEY_BLOCK <= query_start
    )
    whole = one_doc & (block_docs == query_docs[0]) & (block_docs == query_docs[-1])
    kinds = jnp.where(whole, 1, jnp.where(one_doc, 2, 0)).astype(jnp.int32)
    key_docs = docs.reshape(1, token_count)

    def kv_map(i, first, last, start, kind, bdoc):
        return (jnp.minimum(first[0] + i, last[0]), 0)

    def doc_map(i, first, last, start, kind, bdoc):
        return (0, jnp.minimum(first[0] + i, last[0]))

    def fixed(i, first, last, start, kind, bdoc):
        return (0, 0)

    grid_spec = pltpu.PrefetchScalarGridSpec(
        num_scalar_prefetch=5,
        grid=(steps,),
        in_specs=[
            pl.BlockSpec((rows, HEAD_DIM), fixed),
            pl.BlockSpec((KEY_BLOCK, joined_kv.shape[1]), kv_map),
            pl.BlockSpec((1, KEY_BLOCK), doc_map),
            pl.BlockSpec((rows, 1), fixed),
        ],
        out_specs=pl.BlockSpec((rows, HEAD_DIM), fixed),
        scratch_shapes=[
            pltpu.VMEM((rows, 1), jnp.float32),
            pltpu.VMEM((rows, 1), jnp.float32),
            pltpu.VMEM((rows, HEAD_DIM), jnp.float32),
        ],
    )
    return pl.pallas_call(
        functools.partial(prefill_kernel, group=group, factor=factor),
        grid_spec=grid_spec,
        out_shape=jax.ShapeDtypeStruct((rows, HEAD_DIM), jnp.bfloat16),
        compiler_params=pltpu.CompilerParams(dimension_semantics=("arbitrary",)),
    )(
        jnp.reshape(first_block, (1,)).astype(jnp.int32),
        jnp.reshape(last_block, (1,)).astype(jnp.int32),
        jnp.reshape(query_start, (1,)).astype(jnp.int32),
        kinds,
        block_docs.astype(jnp.int32),
        q_rows,
        joined_kv,
        key_docs,
        row_docs,
    )


def merge_partials(packed, axis):
    pieces = lax.all_gather(packed, axis, axis=0, tiled=False)
    tops = pieces[..., HEAD_DIM + 1]
    top = jnp.max(tops, axis=0)
    scale = jnp.exp(tops - top[None])
    summed = jnp.sum(pieces[..., : HEAD_DIM + 1] * scale[..., None], axis=0)
    return jnp.concatenate([summed, top[..., None]], axis=-1)


def project_tp(joined, w_out):
    quarter = w_out.shape[1] // 4
    projected = jnp.dot(joined, w_out, preferred_element_type=jnp.float32)
    parts = [projected[:, j * quarter : (j + 1) * quarter] for j in range(4)]
    first_core = lax.axis_index("c") == 0
    send = jnp.stack(
        [jnp.where(first_core, parts[1], parts[0]), jnp.where(first_core, parts[3], parts[2])], axis=1
    )
    keep = jnp.stack(
        [jnp.where(first_core, parts[0], parts[1]), jnp.where(first_core, parts[2], parts[3])], axis=1
    )
    got = lax.ppermute(send, "c", [(0, 1), (1, 0)])
    half = keep + got
    first_x = lax.axis_index("xl") == 0
    send = jnp.where(first_x, half[:, 1], half[:, 0])
    keep = jnp.where(first_x, half[:, 0], half[:, 1])
    got = lax.ppermute(send, "xl", [(0, 1), (1, 0)])
    return keep + got


def on_device(
    q_pre,
    k_pre,
    v_pre,
    docs,
    q_dec,
    k_dec,
    v_dec,
    k_cache,
    v_cache,
    lengths,
    page_map,
    w_out,
    resid_pre,
    resid_dec,
):
    query_rows = q_pre.shape[0]
    local_heads = q_pre.shape[1] // HEAD_DIM
    local_kv = k_pre.shape[1] // HEAD_DIM
    group_size = local_heads // local_kv
    factor = HEAD_DIM ** (-0.5)
    blk_index = (
        lax.axis_index("z") * (lax.axis_size("y") * lax.axis_size("xh"))
        + lax.axis_index("y") * lax.axis_size("xh")
        + lax.axis_index("xh")
    )
    query_start = blk_index * query_rows
    query_docs = lax.dynamic_slice_in_dim(docs, query_start, query_rows, 0)

    joined_kv = jnp.concatenate([k_pre, v_pre], axis=1)
    for axis in ("xh", "y", "z"):
        joined_kv = lax.all_gather(joined_kv, axis, axis=0, tiled=True)

    doc_start = jnp.sum((docs < query_docs[0]).astype(jnp.int32))
    first_block = doc_start // KEY_BLOCK
    last_block = (query_start + query_rows - 1) // KEY_BLOCK

    attn_rows = prefill_attention(
        q_pre.reshape(query_rows * local_heads, HEAD_DIM),
        joined_kv,
        docs,
        query_docs,
        query_start,
        first_block,
        last_block,
        group_size,
        factor,
    )
    attn_pre = attn_rows.reshape(query_rows, local_heads * HEAD_DIM)

    page_count = page_map.shape[1]
    page_owner = page_map[0]
    page_index = page_map[1]
    requests = jnp.arange(DEC, dtype=jnp.int32)
    belongs = page_owner[:, None] == requests[None, :]
    query_pages = jnp.dot(belongs.astype(jnp.bfloat16), q_dec, preferred_element_type=jnp.float32)
    query_pages = query_pages.astype(jnp.bfloat16).reshape(
        page_count, local_kv, group_size, HEAD_DIM
    )
    page_keys = k_cache.reshape(page_count, PAGE, local_kv, HEAD_DIM)
    page_values = v_cache.reshape(page_count, PAGE, local_kv, HEAD_DIM)
    safe_owner = jnp.minimum(page_owner, DEC - 1)
    positions = page_index[:, None] * PAGE + jnp.arange(PAGE, dtype=jnp.int32)[None, :]
    live_rows = (page_owner[:, None] < DEC) & (positions < lengths[safe_owner][:, None])
    live_mask = live_rows[:, None, None, :]
    page_scores = (
        jnp.einsum("pkgd,ptkd->pkgt", query_pages, page_keys, preferred_element_type=jnp.float32)
        * factor
    )
    page_scores = jnp.where(live_mask, page_scores, NEGATIVE)
    page_top = jnp.max(page_scores, axis=-1)
    request_top = jnp.max(jnp.where(belongs[:, :, None, None], page_top[:, None], NEGATIVE), axis=0)
    shared_top = request_top[safe_owner]
    page_weights = jnp.where(live_mask, jnp.exp(page_scores - shared_top[..., None]), 0.0).astype(
        jnp.bfloat16
    )
    page_weights = lax.optimization_barrier(page_weights)
    page_total = jnp.sum(page_weights.astype(jnp.float32), axis=-1)
    page_vector = jnp.einsum(
        "pkgt,ptkd->pkgd", page_weights, page_values, preferred_element_type=jnp.float32
    )
    membership = belongs.astype(jnp.float32)
    request_total = jnp.einsum(
        "pr,pkg->rkg", membership, page_total, precision=lax.Precision.HIGHEST
    )
    request_vector = jnp.einsum(
        "pr,pkgd->rkgd", membership, page_vector, precision=lax.Precision.HIGHEST
    )
    packed = jnp.concatenate(
        [request_vector, request_total[..., None], request_top[..., None]], axis=-1
    )
    for axis in ("xh", "y", "z"):
        packed = merge_partials(packed, axis)
    merged_vector = packed[..., :HEAD_DIM]
    merged_total = packed[..., HEAD_DIM]
    merged_top = packed[..., HEAD_DIM + 1]

    dec_queries = q_dec.reshape(DEC, local_kv, group_size, HEAD_DIM)
    own_scores = (
        jnp.einsum(
            "rkgd,rkd->rkg",
            dec_queries,
            k_dec.reshape(DEC, local_kv, HEAD_DIM),
            preferred_element_type=jnp.float32,
        )
        * factor
    )
    joint_top = jnp.maximum(merged_top, own_scores)
    own_weight = jnp.exp(own_scores - joint_top).astype(jnp.bfloat16)
    own_weight = lax.optimization_barrier(own_weight).astype(jnp.float32)
    carried_scale = jnp.exp(merged_top - joint_top)
    numerator = merged_vector * carried_scale[..., None] + own_weight[..., None] * v_dec.reshape(
        DEC, local_kv, 1, HEAD_DIM
    ).astype(jnp.float32)
    denominator = merged_total * carried_scale + own_weight
    attn_dec = (
        (numerator / denominator[..., None])
        .reshape(DEC, local_heads * HEAD_DIM)
        .astype(jnp.bfloat16)
    )
    joined = jnp.concatenate([attn_pre, attn_dec], axis=0)
    summed = project_tp(joined, w_out)
    out_pre = resid_pre.astype(jnp.float32) + summed[:query_rows]
    out_dec = resid_dec.astype(jnp.float32) + summed[query_rows:]
    return (out_pre, out_dec)


def solution(mesh):
    blk_size, tp_size = mesh.devices.shape
    split_mesh = Mesh(
        mesh.devices.reshape(8, 4, blk_size // 32, 2, tp_size // 2),
        BLK_AXES + TP_AXES,
    )
    blk = BLK_AXES
    tp = TP_AXES
    placed = (
        P(blk, tp),
        P(blk, tp),
        P(blk, tp),
        P(),
        P(None, tp),
        P(None, tp),
        P(None, tp),
        P(blk, tp),
        P(blk, tp),
        P(),
        P(None, blk),
        P(tp, None),
        P(blk, tp),
        P(None, tp),
    )
    return jax.shard_map(
        on_device,
        mesh=split_mesh,
        in_specs=placed,
        out_specs=(P(blk, tp), P(None, tp)),
        check_vma=False,
    )
```

```python
import functools

import jax
import jax.numpy as jnp
from jax import lax
from jax.experimental import pallas as pl
from jax.experimental.pallas import tpu as pltpu
from jax.sharding import Mesh
from jax.sharding import PartitionSpec as P

HEAD_DIM = 128
PAGE = 128
DEC = 12
KEY_BLOCK = 512
LONGEST_DOC = 10240

NEGATIVE = -1e30

BLK_AXES = ("z", "y", "xh")
TP_AXES = ("xl", "c")


def prefill_kernel(
    first_ref, last_ref, start_ref, kind_ref, bdoc_ref, q_ref, kv_ref, kdoc_ref, qdoc_ref, m_in, l_in, acc_in,
    m_ref, l_ref, acc_ref, *, group, factor, half, half_blocks,
):
    step = pl.program_id(0)
    block = first_ref[0] + step
    active = (block <= last_ref[0]) & ((block // half_blocks) % 2 == half)
    clamped = jnp.minimum(block, last_ref[0])
    kind = kind_ref[clamped]

    @pl.when(step == 0)
    def _():
        m_ref[...] = m_in[...]
        l_ref[...] = l_in[...]
        acc_ref[...] = acc_in[...]

    def accumulate(mode):
        kv = kv_ref[...]
        keys = kv[:, :HEAD_DIM]
        values = kv[:, HEAD_DIM:]
        rows = q_ref.shape[0]
        scores = lax.dot_general(
            q_ref[...], keys, (((1,), (1,)), ((), ())), preferred_element_type=jnp.float32
        ) * factor
        old_top = m_ref[...]
        if mode == 0:
            query_where = start_ref[0] + lax.broadcasted_iota(jnp.int32, (rows, 1), 0) // group
            key_where = block * KEY_BLOCK + lax.broadcasted_iota(jnp.int32, (1, KEY_BLOCK), 1)
            visible = (qdoc_ref[...] == kdoc_ref[...]) & (key_where <= query_where)
            scores = jnp.where(visible, scores, NEGATIVE)
            new_top = jnp.maximum(old_top, jnp.max(scores, axis=1, keepdims=True))
            weights = jnp.where(visible, jnp.exp(scores - new_top), 0.0).astype(jnp.bfloat16)
        else:
            new_top = jnp.maximum(old_top, jnp.max(scores, axis=1, keepdims=True))
            weights = jnp.exp(scores - new_top).astype(jnp.bfloat16)
        rescale = jnp.exp(old_top - new_top)
        new_total = l_ref[...] * rescale + jnp.sum(weights.astype(jnp.float32), axis=1, keepdims=True)
        new_vector = acc_ref[...] * rescale + jnp.dot(
            weights, values, preferred_element_type=jnp.float32
        )
        if mode == 2:
            seen = qdoc_ref[...] == bdoc_ref[clamped]
            new_top = jnp.where(seen, new_top, old_top)
            new_total = jnp.where(seen, new_total, l_ref[...])
            new_vector = jnp.where(seen, new_vector, acc_ref[...])
        l_ref[...] = new_total
        acc_ref[...] = new_vector
        m_ref[...] = new_top

    for mode in (0, 1, 2):

        @pl.when(active & (kind == mode))
        def _():
            accumulate(mode)


def prefill_attention(q_rows, halves, docs, query_docs, query_start, first_block, last_block, group, factor):
    rows = q_rows.shape[0]
    token_count = docs.shape[0]
    group_blocks = 2 * halves[0].shape[0] // (KEY_BLOCK * lax.axis_size("z"))
    half_blocks = group_blocks // 2
    steps = min(
        token_count // KEY_BLOCK,
        (LONGEST_DOC - 1 + rows // group - 1) // KEY_BLOCK + 2,
    )
    row_docs = jnp.repeat(query_docs, group)[:, None]
    block_ids = jnp.arange(token_count // KEY_BLOCK, dtype=jnp.int32)
    block_docs = docs[::KEY_BLOCK]
    one_doc = (block_docs == docs[KEY_BLOCK - 1 :: KEY_BLOCK]) & (
        (block_ids + 1) * KEY_BLOCK <= query_start
    )
    whole = one_doc & (block_docs == query_docs[0]) & (block_docs == query_docs[-1])
    kinds = jnp.where(whole, 1, jnp.where(one_doc, 2, 0)).astype(jnp.int32)
    key_docs = docs.reshape(1, token_count)

    def kv_map(i, first, last, start, kind, bdoc):
        block = jnp.minimum(first[0] + i, last[0])
        return ((block // group_blocks) * half_blocks + block % half_blocks, 0)

    def doc_map(i, first, last, start, kind, bdoc):
        return (0, jnp.minimum(first[0] + i, last[0]))

    def fixed(i, first, last, start, kind, bdoc):
        return (0, 0)

    state_specs = [
        pl.BlockSpec((rows, 1), fixed),
        pl.BlockSpec((rows, 1), fixed),
        pl.BlockSpec((rows, HEAD_DIM), fixed),
    ]
    grid_spec = pltpu.PrefetchScalarGridSpec(
        num_scalar_prefetch=5,
        grid=(steps,),
        in_specs=[
            pl.BlockSpec((rows, HEAD_DIM), fixed),
            pl.BlockSpec((KEY_BLOCK, halves[0].shape[1]), kv_map),
            pl.BlockSpec((1, KEY_BLOCK), doc_map),
            pl.BlockSpec((rows, 1), fixed),
        ]
        + state_specs,
        out_specs=state_specs,
    )
    scalars = (
        jnp.reshape(first_block, (1,)).astype(jnp.int32),
        jnp.reshape(last_block, (1,)).astype(jnp.int32),
        jnp.reshape(query_start, (1,)).astype(jnp.int32),
        kinds,
        block_docs.astype(jnp.int32),
    )
    state = (
        jnp.full((rows, 1), NEGATIVE, jnp.float32),
        jnp.zeros((rows, 1), jnp.float32),
        jnp.zeros((rows, HEAD_DIM), jnp.float32),
    )
    for half, kv_half in enumerate(halves):
        state = pl.pallas_call(
            functools.partial(
                prefill_kernel, group=group, factor=factor, half=half, half_blocks=half_blocks
            ),
            grid_spec=grid_spec,
            out_shape=[jax.ShapeDtypeStruct(part.shape, jnp.float32) for part in state],
            compiler_params=pltpu.CompilerParams(dimension_semantics=("arbitrary",)),
        )(*scalars, q_rows, kv_half, key_docs, row_docs, *state)
    final_top, final_total, final_vector = state
    return (final_vector / final_total).astype(jnp.bfloat16)


def merge_partials(packed, axis):
    pieces = lax.all_gather(packed, axis, axis=0, tiled=False)
    tops = pieces[..., HEAD_DIM + 1]
    top = jnp.max(tops, axis=0)
    scale = jnp.exp(tops - top[None])
    summed = jnp.sum(pieces[..., : HEAD_DIM + 1] * scale[..., None], axis=0)
    return jnp.concatenate([summed, top[..., None]], axis=-1)


def project_tp(joined, w_out):
    quarter = w_out.shape[1] // 4
    projected = jnp.dot(joined, w_out, preferred_element_type=jnp.float32)
    parts = [projected[:, j * quarter : (j + 1) * quarter] for j in range(4)]
    first_core = lax.axis_index("c") == 0
    send = jnp.stack(
        [jnp.where(first_core, parts[1], parts[0]), jnp.where(first_core, parts[3], parts[2])], axis=1
    )
    keep = jnp.stack(
        [jnp.where(first_core, parts[0], parts[1]), jnp.where(first_core, parts[2], parts[3])], axis=1
    )
    got = lax.ppermute(send, "c", [(0, 1), (1, 0)])
    half = keep + got
    first_x = lax.axis_index("xl") == 0
    send = jnp.where(first_x, half[:, 1], half[:, 0])
    keep = jnp.where(first_x, half[:, 0], half[:, 1])
    got = lax.ppermute(send, "xl", [(0, 1), (1, 0)])
    return keep + got


def on_device(
    q_pre,
    k_pre,
    v_pre,
    docs,
    q_dec,
    k_dec,
    v_dec,
    k_cache,
    v_cache,
    lengths,
    page_map,
    w_out,
    resid_pre,
    resid_dec,
):
    query_rows = q_pre.shape[0]
    local_heads = q_pre.shape[1] // HEAD_DIM
    local_kv = k_pre.shape[1] // HEAD_DIM
    group_size = local_heads // local_kv
    factor = HEAD_DIM ** (-0.5)
    blk_index = (
        lax.axis_index("z") * (lax.axis_size("y") * lax.axis_size("xh"))
        + lax.axis_index("y") * lax.axis_size("xh")
        + lax.axis_index("xh")
    )
    query_start = blk_index * query_rows
    query_docs = lax.dynamic_slice_in_dim(docs, query_start, query_rows, 0)

    joined_kv = jnp.concatenate([k_pre, v_pre], axis=1)
    for axis in ("xh", "y"):
        joined_kv = lax.all_gather(joined_kv, axis, axis=0, tiled=True)
    split = joined_kv.shape[0] // 2
    halves = [
        lax.all_gather(joined_kv[:split], "z", axis=0, tiled=True),
        lax.all_gather(joined_kv[split:], "z", axis=0, tiled=True),
    ]

    doc_start = jnp.sum((docs < query_docs[0]).astype(jnp.int32))
    first_block = doc_start // KEY_BLOCK
    last_block = (query_start + query_rows - 1) // KEY_BLOCK

    attn_rows = prefill_attention(
        q_pre.reshape(query_rows * local_heads, HEAD_DIM),
        halves,
        docs,
        query_docs,
        query_start,
        first_block,
        last_block,
        group_size,
        factor,
    )
    attn_pre = attn_rows.reshape(query_rows, local_heads * HEAD_DIM)

    page_count = page_map.shape[1]
    page_owner = page_map[0]
    page_index = page_map[1]
    requests = jnp.arange(DEC, dtype=jnp.int32)
    belongs = page_owner[:, None] == requests[None, :]
    query_pages = jnp.dot(belongs.astype(jnp.bfloat16), q_dec, preferred_element_type=jnp.float32)
    query_pages = query_pages.astype(jnp.bfloat16).reshape(
        page_count, local_kv, group_size, HEAD_DIM
    )
    page_keys = k_cache.reshape(page_count, PAGE, local_kv, HEAD_DIM)
    page_values = v_cache.reshape(page_count, PAGE, local_kv, HEAD_DIM)
    safe_owner = jnp.minimum(page_owner, DEC - 1)
    positions = page_index[:, None] * PAGE + jnp.arange(PAGE, dtype=jnp.int32)[None, :]
    live_rows = (page_owner[:, None] < DEC) & (positions < lengths[safe_owner][:, None])
    live_mask = live_rows[:, None, None, :]
    page_scores = (
        jnp.einsum("pkgd,ptkd->pkgt", query_pages, page_keys, preferred_element_type=jnp.float32)
        * factor
    )
    page_scores = jnp.where(live_mask, page_scores, NEGATIVE)
    page_top = jnp.max(page_scores, axis=-1)
    request_top = jnp.max(jnp.where(belongs[:, :, None, None], page_top[:, None], NEGATIVE), axis=0)
    shared_top = request_top[safe_owner]
    page_weights = jnp.where(live_mask, jnp.exp(page_scores - shared_top[..., None]), 0.0).astype(
        jnp.bfloat16
    )
    page_weights = lax.optimization_barrier(page_weights)
    page_total = jnp.sum(page_weights.astype(jnp.float32), axis=-1)
    page_vector = jnp.einsum(
        "pkgt,ptkd->pkgd", page_weights, page_values, preferred_element_type=jnp.float32
    )
    membership = belongs.astype(jnp.float32)
    request_total = jnp.einsum(
        "pr,pkg->rkg", membership, page_total, precision=lax.Precision.HIGHEST
    )
    request_vector = jnp.einsum(
        "pr,pkgd->rkgd", membership, page_vector, precision=lax.Precision.HIGHEST
    )
    packed = jnp.concatenate(
        [request_vector, request_total[..., None], request_top[..., None]], axis=-1
    )
    for axis in ("xh", "y", "z"):
        packed = merge_partials(packed, axis)
    merged_vector = packed[..., :HEAD_DIM]
    merged_total = packed[..., HEAD_DIM]
    merged_top = packed[..., HEAD_DIM + 1]

    dec_queries = q_dec.reshape(DEC, local_kv, group_size, HEAD_DIM)
    own_scores = (
        jnp.einsum(
            "rkgd,rkd->rkg",
            dec_queries,
            k_dec.reshape(DEC, local_kv, HEAD_DIM),
            preferred_element_type=jnp.float32,
        )
        * factor
    )
    joint_top = jnp.maximum(merged_top, own_scores)
    own_weight = jnp.exp(own_scores - joint_top).astype(jnp.bfloat16)
    own_weight = lax.optimization_barrier(own_weight).astype(jnp.float32)
    carried_scale = jnp.exp(merged_top - joint_top)
    numerator = merged_vector * carried_scale[..., None] + own_weight[..., None] * v_dec.reshape(
        DEC, local_kv, 1, HEAD_DIM
    ).astype(jnp.float32)
    denominator = merged_total * carried_scale + own_weight
    attn_dec = (
        (numerator / denominator[..., None])
        .reshape(DEC, local_heads * HEAD_DIM)
        .astype(jnp.bfloat16)
    )
    joined = jnp.concatenate([attn_pre, attn_dec], axis=0)
    summed = project_tp(joined, w_out)
    out_pre = resid_pre.astype(jnp.float32) + summed[:query_rows]
    out_dec = resid_dec.astype(jnp.float32) + summed[query_rows:]
    return (out_pre, out_dec)


def solution(mesh):
    blk_size, tp_size = mesh.devices.shape
    split_mesh = Mesh(
        mesh.devices.reshape(8, 4, blk_size // 32, 2, tp_size // 2),
        BLK_AXES + TP_AXES,
    )
    blk = BLK_AXES
    tp = TP_AXES
    placed = (
        P(blk, tp),
        P(blk, tp),
        P(blk, tp),
        P(),
        P(None, tp),
        P(None, tp),
        P(None, tp),
        P(blk, tp),
        P(blk, tp),
        P(),
        P(None, blk),
        P(tp, None),
        P(blk, tp),
        P(None, tp),
    )
    return jax.shard_map(
        on_device,
        mesh=split_mesh,
        in_specs=placed,
        out_specs=(P(blk, tp), P(None, tp)),
        check_vma=False,
    )
```

```python
import functools

import jax
import jax.numpy as jnp
from jax import lax
from jax.experimental import pallas as pl
from jax.experimental.pallas import tpu as pltpu
from jax.sharding import Mesh
from jax.sharding import PartitionSpec as P

HEAD_DIM = 128
PAGE = 128
DEC = 12
KEY_BLOCK = 512
LONGEST_DOC = 10240
ROW_CHUNK = 128

NEGATIVE = -1e30

BLK_AXES = ("z", "y", "xh")
TP_AXES = ("xl", "c")


def prefill_kernel(
    first_ref, last_ref, start_ref, kind_ref, bdoc_ref, q_ref, kv_ref, kdoc_ref, qdoc_ref, m_in, l_in, acc_in,
    m_ref, l_ref, acc_ref, *, group, factor, half, half_blocks,
):
    step = pl.program_id(0)
    block = first_ref[0] + step
    active = (block <= last_ref[0]) & ((block // half_blocks) % 2 == half)
    clamped = jnp.minimum(block, last_ref[0])
    kind = kind_ref[clamped]

    @pl.when(step == 0)
    def _():
        m_ref[...] = m_in[...]
        l_ref[...] = l_in[...]
        acc_ref[...] = acc_in[...]

    def accumulate(mode):
        def chunk(index, carried):
            first_row = pl.multiple_of(index * ROW_CHUNK, ROW_CHUNK)
            span = pl.ds(first_row, ROW_CHUNK)
            scores = lax.dot_general(
                q_ref[span, :],
                kv_ref[:, :HEAD_DIM],
                (((1,), (1,)), ((), ())),
                preferred_element_type=jnp.float32,
            ) * factor
            old_top = m_ref[span, :]
            old_total = l_ref[span, :]
            old_vector = acc_ref[span, :]
            row_docs = qdoc_ref[span, :]
            if mode == 0:
                query_where = (
                    start_ref[0]
                    + (first_row + lax.broadcasted_iota(jnp.int32, (ROW_CHUNK, 1), 0)) // group
                )
                key_where = block * KEY_BLOCK + lax.broadcasted_iota(jnp.int32, (1, KEY_BLOCK), 1)
                visible = (row_docs == kdoc_ref[...]) & (key_where <= query_where)
                scores = jnp.where(visible, scores, NEGATIVE)
                new_top = jnp.maximum(old_top, jnp.max(scores, axis=1, keepdims=True))
                weights = jnp.where(visible, jnp.exp(scores - new_top), 0.0).astype(jnp.bfloat16)
            else:
                new_top = jnp.maximum(old_top, jnp.max(scores, axis=1, keepdims=True))
                weights = jnp.exp(scores - new_top).astype(jnp.bfloat16)
            rescale = jnp.exp(old_top - new_top)
            new_total = old_total * rescale + jnp.sum(
                weights.astype(jnp.float32), axis=1, keepdims=True
            )
            new_vector = old_vector * rescale + jnp.dot(
                weights, kv_ref[:, HEAD_DIM:], preferred_element_type=jnp.float32
            )
            if mode == 2:
                seen = row_docs == bdoc_ref[clamped]
                new_top = jnp.where(seen, new_top, old_top)
                new_total = jnp.where(seen, new_total, old_total)
                new_vector = jnp.where(seen, new_vector, old_vector)
            l_ref[span, :] = new_total
            acc_ref[span, :] = new_vector
            m_ref[span, :] = new_top
            return carried

        lax.fori_loop(0, q_ref.shape[0] // ROW_CHUNK, chunk, 0)

    for mode in (0, 1, 2):

        @pl.when(active & (kind == mode))
        def _():
            accumulate(mode)


def prefill_attention(q_rows, halves, docs, query_docs, query_start, first_block, last_block, group, factor):
    rows = q_rows.shape[0]
    token_count = docs.shape[0]
    group_blocks = 2 * halves[0].shape[0] // (KEY_BLOCK * lax.axis_size("z"))
    half_blocks = group_blocks // 2
    steps = min(
        token_count // KEY_BLOCK,
        (LONGEST_DOC - 1 + rows // group - 1) // KEY_BLOCK + 2,
    )
    row_docs = jnp.repeat(query_docs, group)[:, None]
    block_ids = jnp.arange(token_count // KEY_BLOCK, dtype=jnp.int32)
    block_docs = docs[::KEY_BLOCK]
    one_doc = (block_docs == docs[KEY_BLOCK - 1 :: KEY_BLOCK]) & (
        (block_ids + 1) * KEY_BLOCK <= query_start
    )
    whole = one_doc & (block_docs == query_docs[0]) & (block_docs == query_docs[-1])
    kinds = jnp.where(whole, 1, jnp.where(one_doc, 2, 0)).astype(jnp.int32)
    key_docs = docs.reshape(1, token_count)

    def kv_map(i, first, last, start, kind, bdoc):
        block = jnp.minimum(first[0] + i, last[0])
        return ((block // group_blocks) * half_blocks + block % half_blocks, 0)

    def doc_map(i, first, last, start, kind, bdoc):
        return (0, jnp.minimum(first[0] + i, last[0]))

    def fixed(i, first, last, start, kind, bdoc):
        return (0, 0)

    state_specs = [
        pl.BlockSpec((rows, 1), fixed),
        pl.BlockSpec((rows, 1), fixed),
        pl.BlockSpec((rows, HEAD_DIM), fixed),
    ]
    grid_spec = pltpu.PrefetchScalarGridSpec(
        num_scalar_prefetch=5,
        grid=(steps,),
        in_specs=[
            pl.BlockSpec((rows, HEAD_DIM), fixed),
            pl.BlockSpec((KEY_BLOCK, halves[0].shape[1]), kv_map),
            pl.BlockSpec((1, KEY_BLOCK), doc_map),
            pl.BlockSpec((rows, 1), fixed),
        ]
        + state_specs,
        out_specs=state_specs,
    )
    scalars = (
        jnp.reshape(first_block, (1,)).astype(jnp.int32),
        jnp.reshape(last_block, (1,)).astype(jnp.int32),
        jnp.reshape(query_start, (1,)).astype(jnp.int32),
        kinds,
        block_docs.astype(jnp.int32),
    )
    state = (
        jnp.full((rows, 1), NEGATIVE, jnp.float32),
        jnp.zeros((rows, 1), jnp.float32),
        jnp.zeros((rows, HEAD_DIM), jnp.float32),
    )
    for half, kv_half in enumerate(halves):
        state = pl.pallas_call(
            functools.partial(
                prefill_kernel, group=group, factor=factor, half=half, half_blocks=half_blocks
            ),
            grid_spec=grid_spec,
            out_shape=[jax.ShapeDtypeStruct(part.shape, jnp.float32) for part in state],
            compiler_params=pltpu.CompilerParams(dimension_semantics=("arbitrary",)),
        )(*scalars, q_rows, kv_half, key_docs, row_docs, *state)
    final_top, final_total, final_vector = state
    return (final_vector / final_total).astype(jnp.bfloat16)


def merge_partials(packed, axis):
    pieces = lax.all_gather(packed, axis, axis=0, tiled=False)
    tops = pieces[..., HEAD_DIM + 1]
    top = jnp.max(tops, axis=0)
    scale = jnp.exp(tops - top[None])
    summed = jnp.sum(pieces[..., : HEAD_DIM + 1] * scale[..., None], axis=0)
    return jnp.concatenate([summed, top[..., None]], axis=-1)


def project_tp(joined, w_out):
    quarter = w_out.shape[1] // 4
    projected = jnp.dot(joined, w_out, preferred_element_type=jnp.float32)
    parts = [projected[:, j * quarter : (j + 1) * quarter] for j in range(4)]
    first_core = lax.axis_index("c") == 0
    send = jnp.stack(
        [jnp.where(first_core, parts[1], parts[0]), jnp.where(first_core, parts[3], parts[2])], axis=1
    )
    keep = jnp.stack(
        [jnp.where(first_core, parts[0], parts[1]), jnp.where(first_core, parts[2], parts[3])], axis=1
    )
    got = lax.ppermute(send, "c", [(0, 1), (1, 0)])
    half = keep + got
    first_x = lax.axis_index("xl") == 0
    send = jnp.where(first_x, half[:, 1], half[:, 0])
    keep = jnp.where(first_x, half[:, 0], half[:, 1])
    got = lax.ppermute(send, "xl", [(0, 1), (1, 0)])
    return keep + got


def on_device(
    q_pre,
    k_pre,
    v_pre,
    docs,
    q_dec,
    k_dec,
    v_dec,
    k_cache,
    v_cache,
    lengths,
    page_map,
    w_out,
    resid_pre,
    resid_dec,
):
    query_rows = q_pre.shape[0]
    local_heads = q_pre.shape[1] // HEAD_DIM
    local_kv = k_pre.shape[1] // HEAD_DIM
    group_size = local_heads // local_kv
    factor = HEAD_DIM ** (-0.5)
    blk_index = (
        lax.axis_index("z") * (lax.axis_size("y") * lax.axis_size("xh"))
        + lax.axis_index("y") * lax.axis_size("xh")
        + lax.axis_index("xh")
    )
    query_start = blk_index * query_rows
    query_docs = lax.dynamic_slice_in_dim(docs, query_start, query_rows, 0)

    joined_kv = jnp.concatenate([k_pre, v_pre], axis=1)
    for axis in ("xh", "y"):
        joined_kv = lax.all_gather(joined_kv, axis, axis=0, tiled=True)
    split = joined_kv.shape[0] // 2
    halves = [
        lax.all_gather(joined_kv[:split], "z", axis=0, tiled=True),
        lax.all_gather(joined_kv[split:], "z", axis=0, tiled=True),
    ]

    doc_start = jnp.sum((docs < query_docs[0]).astype(jnp.int32))
    first_block = doc_start // KEY_BLOCK
    last_block = (query_start + query_rows - 1) // KEY_BLOCK

    attn_rows = prefill_attention(
        q_pre.reshape(query_rows * local_heads, HEAD_DIM),
        halves,
        docs,
        query_docs,
        query_start,
        first_block,
        last_block,
        group_size,
        factor,
    )
    attn_pre = attn_rows.reshape(query_rows, local_heads * HEAD_DIM)

    page_count = page_map.shape[1]
    page_owner = page_map[0]
    page_index = page_map[1]
    requests = jnp.arange(DEC, dtype=jnp.int32)
    belongs = page_owner[:, None] == requests[None, :]
    query_pages = jnp.dot(belongs.astype(jnp.bfloat16), q_dec, preferred_element_type=jnp.float32)
    query_pages = query_pages.astype(jnp.bfloat16).reshape(
        page_count, local_kv, group_size, HEAD_DIM
    )
    page_keys = k_cache.reshape(page_count, PAGE, local_kv, HEAD_DIM)
    page_values = v_cache.reshape(page_count, PAGE, local_kv, HEAD_DIM)
    safe_owner = jnp.minimum(page_owner, DEC - 1)
    positions = page_index[:, None] * PAGE + jnp.arange(PAGE, dtype=jnp.int32)[None, :]
    live_rows = (page_owner[:, None] < DEC) & (positions < lengths[safe_owner][:, None])
    live_mask = live_rows[:, None, None, :]
    page_scores = (
        jnp.einsum("pkgd,ptkd->pkgt", query_pages, page_keys, preferred_element_type=jnp.float32)
        * factor
    )
    page_scores = jnp.where(live_mask, page_scores, NEGATIVE)
    page_top = jnp.max(page_scores, axis=-1)
    request_top = jnp.max(jnp.where(belongs[:, :, None, None], page_top[:, None], NEGATIVE), axis=0)
    shared_top = request_top[safe_owner]
    page_weights = jnp.where(live_mask, jnp.exp(page_scores - shared_top[..., None]), 0.0).astype(
        jnp.bfloat16
    )
    page_weights = lax.optimization_barrier(page_weights)
    page_total = jnp.sum(page_weights.astype(jnp.float32), axis=-1)
    page_vector = jnp.einsum(
        "pkgt,ptkd->pkgd", page_weights, page_values, preferred_element_type=jnp.float32
    )
    membership = belongs.astype(jnp.float32)
    request_total = jnp.einsum(
        "pr,pkg->rkg", membership, page_total, precision=lax.Precision.HIGHEST
    )
    request_vector = jnp.einsum(
        "pr,pkgd->rkgd", membership, page_vector, precision=lax.Precision.HIGHEST
    )
    packed = jnp.concatenate(
        [request_vector, request_total[..., None], request_top[..., None]], axis=-1
    )
    for axis in ("xh", "y", "z"):
        packed = merge_partials(packed, axis)
    merged_vector = packed[..., :HEAD_DIM]
    merged_total = packed[..., HEAD_DIM]
    merged_top = packed[..., HEAD_DIM + 1]

    dec_queries = q_dec.reshape(DEC, local_kv, group_size, HEAD_DIM)
    own_scores = (
        jnp.einsum(
            "rkgd,rkd->rkg",
            dec_queries,
            k_dec.reshape(DEC, local_kv, HEAD_DIM),
            preferred_element_type=jnp.float32,
        )
        * factor
    )
    joint_top = jnp.maximum(merged_top, own_scores)
    own_weight = jnp.exp(own_scores - joint_top).astype(jnp.bfloat16)
    own_weight = lax.optimization_barrier(own_weight).astype(jnp.float32)
    carried_scale = jnp.exp(merged_top - joint_top)
    numerator = merged_vector * carried_scale[..., None] + own_weight[..., None] * v_dec.reshape(
        DEC, local_kv, 1, HEAD_DIM
    ).astype(jnp.float32)
    denominator = merged_total * carried_scale + own_weight
    attn_dec = (
        (numerator / denominator[..., None])
        .reshape(DEC, local_heads * HEAD_DIM)
        .astype(jnp.bfloat16)
    )
    joined = jnp.concatenate([attn_pre, attn_dec], axis=0)
    summed = project_tp(joined, w_out)
    out_pre = resid_pre.astype(jnp.float32) + summed[:query_rows]
    out_dec = resid_dec.astype(jnp.float32) + summed[query_rows:]
    return (out_pre, out_dec)


def solution(mesh):
    blk_size, tp_size = mesh.devices.shape
    split_mesh = Mesh(
        mesh.devices.reshape(8, 4, blk_size // 32, 2, tp_size // 2),
        BLK_AXES + TP_AXES,
    )
    blk = BLK_AXES
    tp = TP_AXES
    placed = (
        P(blk, tp),
        P(blk, tp),
        P(blk, tp),
        P(),
        P(None, tp),
        P(None, tp),
        P(None, tp),
        P(blk, tp),
        P(blk, tp),
        P(),
        P(None, blk),
        P(tp, None),
        P(blk, tp),
        P(None, tp),
    )
    return jax.shard_map(
        on_device,
        mesh=split_mesh,
        in_specs=placed,
        out_specs=(P(blk, tp), P(None, tp)),
        check_vma=False,
    )
```

```python
import functools

import jax
import jax.numpy as jnp
from jax import lax
from jax.experimental import pallas as pl
from jax.experimental.pallas import tpu as pltpu
from jax.sharding import Mesh
from jax.sharding import PartitionSpec as P

HEAD_DIM = 128
PAGE = 128
DEC = 12
KEY_BLOCK = 512
LONGEST_DOC = 10240

NEGATIVE = -1e30

BLK_AXES = ("z", "y", "xh")
TP_AXES = ("xl", "c")


def prefill_kernel(
    first_ref, last_ref, start_ref, kind_ref, bdoc_ref, q_ref, kv_ref, kdoc_ref, qdoc_ref, m_in, l_in, acc_in,
    m_ref, l_ref, acc_ref, *, group, factor, half, half_blocks,
):
    step = pl.program_id(0)
    block = first_ref[0] + step
    active = (block <= last_ref[0]) & ((block // half_blocks) % 2 == half)
    clamped = jnp.minimum(block, last_ref[0])
    kind = kind_ref[clamped]

    @pl.when(step == 0)
    def _():
        m_ref[...] = m_in[...]
        l_ref[...] = l_in[...]
        acc_ref[...] = acc_in[...]

    def accumulate(mode):
        kv = kv_ref[...]
        keys = kv[:, :HEAD_DIM]
        values = kv[:, HEAD_DIM:]
        rows = q_ref.shape[0]
        scores = lax.dot_general(
            q_ref[...], keys, (((1,), (1,)), ((), ())), preferred_element_type=jnp.float32
        ) * factor
        old_top = m_ref[...]
        if mode == 0:
            query_where = start_ref[0] + lax.broadcasted_iota(jnp.int32, (rows, 1), 0) // group
            key_where = block * KEY_BLOCK + lax.broadcasted_iota(jnp.int32, (1, KEY_BLOCK), 1)
            visible = (qdoc_ref[...] == kdoc_ref[...]) & (key_where <= query_where)
            scores = jnp.where(visible, scores, NEGATIVE)
            new_top = jnp.maximum(old_top, jnp.max(scores, axis=1, keepdims=True))
            weights = jnp.where(visible, jnp.exp(scores - new_top), 0.0).astype(jnp.bfloat16)
        else:
            new_top = jnp.maximum(old_top, jnp.max(scores, axis=1, keepdims=True))
            weights = jnp.exp(scores - new_top).astype(jnp.bfloat16)
        rescale = jnp.exp(old_top - new_top)
        new_total = l_ref[...] * rescale + jnp.sum(weights.astype(jnp.float32), axis=1, keepdims=True)
        new_vector = acc_ref[...] * rescale + jnp.dot(
            weights, values, preferred_element_type=jnp.float32
        )
        if mode == 2:
            seen = qdoc_ref[...] == bdoc_ref[clamped]
            new_top = jnp.where(seen, new_top, old_top)
            new_total = jnp.where(seen, new_total, l_ref[...])
            new_vector = jnp.where(seen, new_vector, acc_ref[...])
        l_ref[...] = new_total
        acc_ref[...] = new_vector
        m_ref[...] = new_top

    for mode in (0, 1, 2):

        @pl.when(active & (kind == mode))
        def _():
            accumulate(mode)


def prefill_attention(q_rows, halves, docs, query_docs, query_start, first_block, last_block, group, factor):
    rows = q_rows.shape[0]
    token_count = docs.shape[0]
    group_blocks = 2 * halves[0].shape[0] // (KEY_BLOCK * lax.axis_size("z"))
    half_blocks = group_blocks // 2
    steps = min(
        token_count // KEY_BLOCK,
        (LONGEST_DOC - 1 + rows // group - 1) // KEY_BLOCK + 2,
    )
    row_docs = jnp.repeat(query_docs, group)[:, None]
    block_ids = jnp.arange(token_count // KEY_BLOCK, dtype=jnp.int32)
    block_docs = docs[::KEY_BLOCK]
    one_doc = (block_docs == docs[KEY_BLOCK - 1 :: KEY_BLOCK]) & (
        (block_ids + 1) * KEY_BLOCK <= query_start
    )
    whole = one_doc & (block_docs == query_docs[0]) & (block_docs == query_docs[-1])
    kinds = jnp.where(whole, 1, jnp.where(one_doc, 2, 0)).astype(jnp.int32)
    key_docs = docs.reshape(1, token_count)

    def kv_map(i, first, last, start, kind, bdoc):
        block = jnp.minimum(first[0] + i, last[0])
        return ((block // group_blocks) * half_blocks + block % half_blocks, 0)

    def doc_map(i, first, last, start, kind, bdoc):
        return (0, jnp.minimum(first[0] + i, last[0]))

    def fixed(i, first, last, start, kind, bdoc):
        return (0, 0)

    state_specs = [
        pl.BlockSpec((rows, 1), fixed),
        pl.BlockSpec((rows, 1), fixed),
        pl.BlockSpec((rows, HEAD_DIM), fixed),
    ]
    grid_spec = pltpu.PrefetchScalarGridSpec(
        num_scalar_prefetch=5,
        grid=(steps,),
        in_specs=[
            pl.BlockSpec((rows, HEAD_DIM), fixed),
            pl.BlockSpec((KEY_BLOCK, halves[0].shape[1]), kv_map),
            pl.BlockSpec((1, KEY_BLOCK), doc_map),
            pl.BlockSpec((rows, 1), fixed),
        ]
        + state_specs,
        out_specs=state_specs,
    )
    scalars = (
        jnp.reshape(first_block, (1,)).astype(jnp.int32),
        jnp.reshape(last_block, (1,)).astype(jnp.int32),
        jnp.reshape(query_start, (1,)).astype(jnp.int32),
        kinds,
        block_docs.astype(jnp.int32),
    )
    state = (
        jnp.full((rows, 1), NEGATIVE, jnp.float32),
        jnp.zeros((rows, 1), jnp.float32),
        jnp.zeros((rows, HEAD_DIM), jnp.float32),
    )
    for half, kv_half in enumerate(halves):
        state = pl.pallas_call(
            functools.partial(
                prefill_kernel, group=group, factor=factor, half=half, half_blocks=half_blocks
            ),
            grid_spec=grid_spec,
            out_shape=[jax.ShapeDtypeStruct(part.shape, jnp.float32) for part in state],
            compiler_params=pltpu.CompilerParams(dimension_semantics=("arbitrary",)),
        )(*scalars, q_rows, kv_half, key_docs, row_docs, *state)
    final_top, final_total, final_vector = state
    return (final_vector / final_total).astype(jnp.bfloat16)


def merge_partials(packed, axis):
    pieces = lax.all_gather(packed, axis, axis=0, tiled=False)
    tops = pieces[..., HEAD_DIM + 1]
    top = jnp.max(tops, axis=0)
    scale = jnp.exp(tops - top[None])
    summed = jnp.sum(pieces[..., : HEAD_DIM + 1] * scale[..., None], axis=0)
    return jnp.concatenate([summed, top[..., None]], axis=-1)


def prefetch_weights(w_out):
    half = w_out.shape[1] // 2
    first_x = lax.axis_index("xl") == 0
    keep = jnp.where(first_x, w_out[:, :half], w_out[:, half:])
    send = jnp.where(first_x, w_out[:, half:], w_out[:, :half])
    return keep, lax.ppermute(send, "xl", [(0, 1), (1, 0)])


def project_tp(joined, w_keep, w_partner):
    partner_rows = lax.ppermute(joined, "xl", [(0, 1), (1, 0)])
    partial = jnp.dot(joined, w_keep, preferred_element_type=jnp.float32)
    partial = partial + jnp.dot(partner_rows, w_partner, preferred_element_type=jnp.float32)
    quarter = partial.shape[1] // 2
    first_core = lax.axis_index("c") == 0
    send = jnp.where(first_core, partial[:, quarter:], partial[:, :quarter])
    keep = jnp.where(first_core, partial[:, :quarter], partial[:, quarter:])
    return keep + lax.ppermute(send, "c", [(0, 1), (1, 0)])


def on_device(
    q_pre,
    k_pre,
    v_pre,
    docs,
    q_dec,
    k_dec,
    v_dec,
    k_cache,
    v_cache,
    lengths,
    page_map,
    w_out,
    resid_pre,
    resid_dec,
):
    query_rows = q_pre.shape[0]
    local_heads = q_pre.shape[1] // HEAD_DIM
    local_kv = k_pre.shape[1] // HEAD_DIM
    group_size = local_heads // local_kv
    factor = HEAD_DIM ** (-0.5)
    blk_index = (
        lax.axis_index("z") * (lax.axis_size("y") * lax.axis_size("xh"))
        + lax.axis_index("y") * lax.axis_size("xh")
        + lax.axis_index("xh")
    )
    query_start = blk_index * query_rows
    query_docs = lax.dynamic_slice_in_dim(docs, query_start, query_rows, 0)

    w_keep, w_partner = prefetch_weights(w_out)

    joined_kv = jnp.concatenate([k_pre, v_pre], axis=1)
    for axis in ("xh", "y"):
        joined_kv = lax.all_gather(joined_kv, axis, axis=0, tiled=True)
    split = joined_kv.shape[0] // 2
    halves = [
        lax.all_gather(joined_kv[:split], "z", axis=0, tiled=True),
        lax.all_gather(joined_kv[split:], "z", axis=0, tiled=True),
    ]

    doc_start = jnp.sum((docs < query_docs[0]).astype(jnp.int32))
    first_block = doc_start // KEY_BLOCK
    last_block = (query_start + query_rows - 1) // KEY_BLOCK

    attn_rows = prefill_attention(
        q_pre.reshape(query_rows * local_heads, HEAD_DIM),
        halves,
        docs,
        query_docs,
        query_start,
        first_block,
        last_block,
        group_size,
        factor,
    )
    attn_pre = attn_rows.reshape(query_rows, local_heads * HEAD_DIM)

    page_count = page_map.shape[1]
    page_owner = page_map[0]
    page_index = page_map[1]
    requests = jnp.arange(DEC, dtype=jnp.int32)
    belongs = page_owner[:, None] == requests[None, :]
    query_pages = jnp.dot(belongs.astype(jnp.bfloat16), q_dec, preferred_element_type=jnp.float32)
    query_pages = query_pages.astype(jnp.bfloat16).reshape(
        page_count, local_kv, group_size, HEAD_DIM
    )
    page_keys = k_cache.reshape(page_count, PAGE, local_kv, HEAD_DIM)
    page_values = v_cache.reshape(page_count, PAGE, local_kv, HEAD_DIM)
    safe_owner = jnp.minimum(page_owner, DEC - 1)
    positions = page_index[:, None] * PAGE + jnp.arange(PAGE, dtype=jnp.int32)[None, :]
    live_rows = (page_owner[:, None] < DEC) & (positions < lengths[safe_owner][:, None])
    live_mask = live_rows[:, None, None, :]
    page_scores = (
        jnp.einsum("pkgd,ptkd->pkgt", query_pages, page_keys, preferred_element_type=jnp.float32)
        * factor
    )
    page_scores = jnp.where(live_mask, page_scores, NEGATIVE)
    page_top = jnp.max(page_scores, axis=-1)
    request_top = jnp.max(jnp.where(belongs[:, :, None, None], page_top[:, None], NEGATIVE), axis=0)
    shared_top = request_top[safe_owner]
    page_weights = jnp.where(live_mask, jnp.exp(page_scores - shared_top[..., None]), 0.0).astype(
        jnp.bfloat16
    )
    page_weights = lax.optimization_barrier(page_weights)
    page_total = jnp.sum(page_weights.astype(jnp.float32), axis=-1)
    page_vector = jnp.einsum(
        "pkgt,ptkd->pkgd", page_weights, page_values, preferred_element_type=jnp.float32
    )
    membership = belongs.astype(jnp.float32)
    request_total = jnp.einsum(
        "pr,pkg->rkg", membership, page_total, precision=lax.Precision.HIGHEST
    )
    request_vector = jnp.einsum(
        "pr,pkgd->rkgd", membership, page_vector, precision=lax.Precision.HIGHEST
    )
    packed = jnp.concatenate(
        [request_vector, request_total[..., None], request_top[..., None]], axis=-1
    )
    for axis in ("xh", "y", "z"):
        packed = merge_partials(packed, axis)
    merged_vector = packed[..., :HEAD_DIM]
    merged_total = packed[..., HEAD_DIM]
    merged_top = packed[..., HEAD_DIM + 1]

    dec_queries = q_dec.reshape(DEC, local_kv, group_size, HEAD_DIM)
    own_scores = (
        jnp.einsum(
            "rkgd,rkd->rkg",
            dec_queries,
            k_dec.reshape(DEC, local_kv, HEAD_DIM),
            preferred_element_type=jnp.float32,
        )
        * factor
    )
    joint_top = jnp.maximum(merged_top, own_scores)
    own_weight = jnp.exp(own_scores - joint_top).astype(jnp.bfloat16)
    own_weight = lax.optimization_barrier(own_weight).astype(jnp.float32)
    carried_scale = jnp.exp(merged_top - joint_top)
    numerator = merged_vector * carried_scale[..., None] + own_weight[..., None] * v_dec.reshape(
        DEC, local_kv, 1, HEAD_DIM
    ).astype(jnp.float32)
    denominator = merged_total * carried_scale + own_weight
    attn_dec = (
        (numerator / denominator[..., None])
        .reshape(DEC, local_heads * HEAD_DIM)
        .astype(jnp.bfloat16)
    )
    joined = jnp.concatenate([attn_pre, attn_dec], axis=0)
    summed = project_tp(joined, w_keep, w_partner)
    out_pre = resid_pre.astype(jnp.float32) + summed[:query_rows]
    out_dec = resid_dec.astype(jnp.float32) + summed[query_rows:]
    return (out_pre, out_dec)


def solution(mesh):
    blk_size, tp_size = mesh.devices.shape
    split_mesh = Mesh(
        mesh.devices.reshape(8, 4, blk_size // 32, 2, tp_size // 2),
        BLK_AXES + TP_AXES,
    )
    blk = BLK_AXES
    tp = TP_AXES
    placed = (
        P(blk, tp),
        P(blk, tp),
        P(blk, tp),
        P(),
        P(None, tp),
        P(None, tp),
        P(None, tp),
        P(blk, tp),
        P(blk, tp),
        P(),
        P(None, blk),
        P(tp, None),
        P(blk, tp),
        P(None, tp),
    )
    return jax.shard_map(
        on_device,
        mesh=split_mesh,
        in_specs=placed,
        out_specs=(P(blk, tp), P(None, tp)),
        check_vma=False,
    )
```

```python
import functools

import jax
import jax.numpy as jnp
from jax import lax
from jax.experimental import pallas as pl
from jax.experimental.pallas import tpu as pltpu
from jax.sharding import Mesh
from jax.sharding import PartitionSpec as P

HEAD_DIM = 128
PAGE = 128
DEC = 12
KEY_BLOCK = 512
LONGEST_DOC = 10240

NEGATIVE = -1e30

BLK_AXES = ("z", "y", "xh")
TP_AXES = ("xl", "c")


def prefill_kernel(
    first_ref, last_ref, start_ref, kind_ref, bdoc_ref, q_ref, kv_ref, kdoc_ref, qdoc_ref, m_in, l_in, acc_in,
    m_ref, l_ref, acc_ref, *, group, factor, half, half_blocks,
):
    step = pl.program_id(0)
    block = first_ref[0] + step
    active = (block <= last_ref[0]) & ((block // half_blocks) % 2 == half)
    clamped = jnp.minimum(block, last_ref[0])
    kind = kind_ref[clamped]

    @pl.when(step == 0)
    def _():
        m_ref[...] = m_in[...]
        l_ref[...] = l_in[...]
        acc_ref[...] = acc_in[...]

    def accumulate(mode):
        kv = kv_ref[...]
        keys = kv[:, :HEAD_DIM]
        values = kv[:, HEAD_DIM:]
        rows = q_ref.shape[0]
        scores = lax.dot_general(
            q_ref[...], keys, (((1,), (1,)), ((), ())), preferred_element_type=jnp.float32
        ) * factor
        old_top = m_ref[...]
        if mode == 0:
            query_where = start_ref[0] + lax.broadcasted_iota(jnp.int32, (rows, 1), 0) // group
            key_where = block * KEY_BLOCK + lax.broadcasted_iota(jnp.int32, (1, KEY_BLOCK), 1)
            visible = (qdoc_ref[...] == kdoc_ref[...]) & (key_where <= query_where)
            scores = jnp.where(visible, scores, NEGATIVE)
            new_top = jnp.maximum(old_top, jnp.max(scores, axis=1, keepdims=True))
            weights = jnp.where(visible, jnp.exp(scores - new_top), 0.0).astype(jnp.bfloat16)
        else:
            new_top = jnp.maximum(old_top, jnp.max(scores, axis=1, keepdims=True))
            weights = jnp.exp(scores - new_top).astype(jnp.bfloat16)
        rescale = jnp.exp(old_top - new_top)
        new_total = l_ref[...] * rescale + jnp.sum(weights.astype(jnp.float32), axis=1, keepdims=True)
        new_vector = acc_ref[...] * rescale + jnp.dot(
            weights, values, preferred_element_type=jnp.float32
        )
        if mode == 2:
            seen = qdoc_ref[...] == bdoc_ref[clamped]
            new_top = jnp.where(seen, new_top, old_top)
            new_total = jnp.where(seen, new_total, l_ref[...])
            new_vector = jnp.where(seen, new_vector, acc_ref[...])
        l_ref[...] = new_total
        acc_ref[...] = new_vector
        m_ref[...] = new_top

    for mode in (0, 1, 2):

        @pl.when(active & (kind == mode))
        def _():
            accumulate(mode)


def prefill_attention(q_rows, halves, docs, query_docs, query_start, first_block, last_block, group, factor):
    rows = q_rows.shape[0]
    token_count = docs.shape[0]
    group_blocks = 2 * halves[0].shape[0] // (KEY_BLOCK * lax.axis_size("z"))
    half_blocks = group_blocks // 2
    steps = min(
        token_count // KEY_BLOCK,
        (LONGEST_DOC - 1 + rows // group - 1) // KEY_BLOCK + 2,
    )
    row_docs = jnp.repeat(query_docs, group)[:, None]
    block_ids = jnp.arange(token_count // KEY_BLOCK, dtype=jnp.int32)
    block_docs = docs[::KEY_BLOCK]
    one_doc = (block_docs == docs[KEY_BLOCK - 1 :: KEY_BLOCK]) & (
        (block_ids + 1) * KEY_BLOCK <= query_start
    )
    whole = one_doc & (block_docs == query_docs[0]) & (block_docs == query_docs[-1])
    kinds = jnp.where(whole, 1, jnp.where(one_doc, 2, 0)).astype(jnp.int32)
    key_docs = docs.reshape(1, token_count)

    def kv_map(i, first, last, start, kind, bdoc):
        block = jnp.minimum(first[0] + i, last[0])
        return ((block // group_blocks) * half_blocks + block % half_blocks, 0)

    def doc_map(i, first, last, start, kind, bdoc):
        return (0, jnp.minimum(first[0] + i, last[0]))

    def fixed(i, first, last, start, kind, bdoc):
        return (0, 0)

    state_specs = [
        pl.BlockSpec((rows, 1), fixed),
        pl.BlockSpec((rows, 1), fixed),
        pl.BlockSpec((rows, HEAD_DIM), fixed),
    ]
    grid_spec = pltpu.PrefetchScalarGridSpec(
        num_scalar_prefetch=5,
        grid=(steps,),
        in_specs=[
            pl.BlockSpec((rows, HEAD_DIM), fixed),
            pl.BlockSpec((KEY_BLOCK, halves[0].shape[1]), kv_map),
            pl.BlockSpec((1, KEY_BLOCK), doc_map),
            pl.BlockSpec((rows, 1), fixed),
        ]
        + state_specs,
        out_specs=state_specs,
    )
    scalars = (
        jnp.reshape(first_block, (1,)).astype(jnp.int32),
        jnp.reshape(last_block, (1,)).astype(jnp.int32),
        jnp.reshape(query_start, (1,)).astype(jnp.int32),
        kinds,
        block_docs.astype(jnp.int32),
    )
    state = (
        jnp.full((rows, 1), NEGATIVE, jnp.float32),
        jnp.zeros((rows, 1), jnp.float32),
        jnp.zeros((rows, HEAD_DIM), jnp.float32),
    )
    for half, kv_half in enumerate(halves):
        state = pl.pallas_call(
            functools.partial(
                prefill_kernel, group=group, factor=factor, half=half, half_blocks=half_blocks
            ),
            grid_spec=grid_spec,
            out_shape=[jax.ShapeDtypeStruct(part.shape, jnp.float32) for part in state],
            compiler_params=pltpu.CompilerParams(dimension_semantics=("arbitrary",)),
        )(*scalars, q_rows, kv_half, key_docs, row_docs, *state)
    final_top, final_total, final_vector = state
    return (final_vector / final_total).astype(jnp.bfloat16)


def merge_partials(packed, axis):
    pieces = lax.all_gather(packed, axis, axis=0, tiled=False)
    tops = pieces[..., HEAD_DIM + 1]
    top = jnp.max(tops, axis=0)
    scale = jnp.exp(tops - top[None])
    summed = jnp.sum(pieces[..., : HEAD_DIM + 1] * scale[..., None], axis=0)
    return jnp.concatenate([summed, top[..., None]], axis=-1)


def prefetch_weights(w_out):
    half = w_out.shape[1] // 2
    first_x = lax.axis_index("xl") == 0
    keep = jnp.where(first_x, w_out[:, :half], w_out[:, half:])
    send = jnp.where(first_x, w_out[:, half:], w_out[:, :half])
    return keep, send


def project_tp(joined, w_keep, w_partner):
    partner_rows = lax.ppermute(joined, "xl", [(0, 1), (1, 0)])
    partial = jnp.dot(joined, w_keep, preferred_element_type=jnp.float32)
    partial = partial + jnp.dot(partner_rows, w_partner, preferred_element_type=jnp.float32)
    quarter = partial.shape[1] // 2
    first_core = lax.axis_index("c") == 0
    send = jnp.where(first_core, partial[:, quarter:], partial[:, :quarter])
    keep = jnp.where(first_core, partial[:, :quarter], partial[:, quarter:])
    return keep + lax.ppermute(send, "c", [(0, 1), (1, 0)])


def on_device(
    q_pre,
    k_pre,
    v_pre,
    docs,
    q_dec,
    k_dec,
    v_dec,
    k_cache,
    v_cache,
    lengths,
    page_map,
    w_out,
    resid_pre,
    resid_dec,
):
    query_rows = q_pre.shape[0]
    local_heads = q_pre.shape[1] // HEAD_DIM
    local_kv = k_pre.shape[1] // HEAD_DIM
    group_size = local_heads // local_kv
    factor = HEAD_DIM ** (-0.5)
    blk_index = (
        lax.axis_index("z") * (lax.axis_size("y") * lax.axis_size("xh"))
        + lax.axis_index("y") * lax.axis_size("xh")
        + lax.axis_index("xh")
    )
    query_start = blk_index * query_rows
    query_docs = lax.dynamic_slice_in_dim(docs, query_start, query_rows, 0)

    w_keep, w_send = prefetch_weights(w_out)

    joined_kv = jnp.concatenate([k_pre, v_pre], axis=1)
    for axis in ("xh", "y"):
        joined_kv = lax.all_gather(joined_kv, axis, axis=0, tiled=True)
    split = joined_kv.shape[0] // 2
    halves = [
        lax.all_gather(joined_kv[:split], "z", axis=0, tiled=True),
        lax.all_gather(joined_kv[split:], "z", axis=0, tiled=True),
    ]

    doc_start = jnp.sum((docs < query_docs[0]).astype(jnp.int32))
    first_block = doc_start // KEY_BLOCK
    last_block = (query_start + query_rows - 1) // KEY_BLOCK

    attn_rows = prefill_attention(
        q_pre.reshape(query_rows * local_heads, HEAD_DIM),
        halves,
        docs,
        query_docs,
        query_start,
        first_block,
        last_block,
        group_size,
        factor,
    )
    attn_pre = attn_rows.reshape(query_rows, local_heads * HEAD_DIM)

    page_count = page_map.shape[1]
    page_owner = page_map[0]
    page_index = page_map[1]
    requests = jnp.arange(DEC, dtype=jnp.int32)
    belongs = page_owner[:, None] == requests[None, :]
    query_pages = jnp.dot(belongs.astype(jnp.bfloat16), q_dec, preferred_element_type=jnp.float32)
    query_pages = query_pages.astype(jnp.bfloat16).reshape(
        page_count, local_kv, group_size, HEAD_DIM
    )
    page_keys = k_cache.reshape(page_count, PAGE, local_kv, HEAD_DIM)
    page_values = v_cache.reshape(page_count, PAGE, local_kv, HEAD_DIM)
    safe_owner = jnp.minimum(page_owner, DEC - 1)
    positions = page_index[:, None] * PAGE + jnp.arange(PAGE, dtype=jnp.int32)[None, :]
    live_rows = (page_owner[:, None] < DEC) & (positions < lengths[safe_owner][:, None])
    live_mask = live_rows[:, None, None, :]
    page_scores = (
        jnp.einsum("pkgd,ptkd->pkgt", query_pages, page_keys, preferred_element_type=jnp.float32)
        * factor
    )
    page_scores = jnp.where(live_mask, page_scores, NEGATIVE)
    page_top = jnp.max(page_scores, axis=-1)
    request_top = jnp.max(jnp.where(belongs[:, :, None, None], page_top[:, None], NEGATIVE), axis=0)
    shared_top = request_top[safe_owner]
    page_weights = jnp.where(live_mask, jnp.exp(page_scores - shared_top[..., None]), 0.0).astype(
        jnp.bfloat16
    )
    page_weights = lax.optimization_barrier(page_weights)
    page_total = jnp.sum(page_weights.astype(jnp.float32), axis=-1)
    page_vector = jnp.einsum(
        "pkgt,ptkd->pkgd", page_weights, page_values, preferred_element_type=jnp.float32
    )
    membership = belongs.astype(jnp.float32)
    request_total = jnp.einsum(
        "pr,pkg->rkg", membership, page_total, precision=lax.Precision.HIGHEST
    )
    request_vector = jnp.einsum(
        "pr,pkgd->rkgd", membership, page_vector, precision=lax.Precision.HIGHEST
    )
    packed = jnp.concatenate(
        [request_vector, request_total[..., None], request_top[..., None]], axis=-1
    )
    for axis in ("xh", "y", "z"):
        packed = merge_partials(packed, axis)
    packed, w_send = lax.optimization_barrier((packed, w_send))
    w_partner = lax.ppermute(w_send, "xl", [(0, 1), (1, 0)])
    merged_vector = packed[..., :HEAD_DIM]
    merged_total = packed[..., HEAD_DIM]
    merged_top = packed[..., HEAD_DIM + 1]

    dec_queries = q_dec.reshape(DEC, local_kv, group_size, HEAD_DIM)
    own_scores = (
        jnp.einsum(
            "rkgd,rkd->rkg",
            dec_queries,
            k_dec.reshape(DEC, local_kv, HEAD_DIM),
            preferred_element_type=jnp.float32,
        )
        * factor
    )
    joint_top = jnp.maximum(merged_top, own_scores)
    own_weight = jnp.exp(own_scores - joint_top).astype(jnp.bfloat16)
    own_weight = lax.optimization_barrier(own_weight).astype(jnp.float32)
    carried_scale = jnp.exp(merged_top - joint_top)
    numerator = merged_vector * carried_scale[..., None] + own_weight[..., None] * v_dec.reshape(
        DEC, local_kv, 1, HEAD_DIM
    ).astype(jnp.float32)
    denominator = merged_total * carried_scale + own_weight
    attn_dec = (
        (numerator / denominator[..., None])
        .reshape(DEC, local_heads * HEAD_DIM)
        .astype(jnp.bfloat16)
    )
    joined = jnp.concatenate([attn_pre, attn_dec], axis=0)
    summed = project_tp(joined, w_keep, w_partner)
    out_pre = resid_pre.astype(jnp.float32) + summed[:query_rows]
    out_dec = resid_dec.astype(jnp.float32) + summed[query_rows:]
    return (out_pre, out_dec)


def solution(mesh):
    blk_size, tp_size = mesh.devices.shape
    split_mesh = Mesh(
        mesh.devices.reshape(8, 4, blk_size // 32, 2, tp_size // 2),
        BLK_AXES + TP_AXES,
    )
    blk = BLK_AXES
    tp = TP_AXES
    placed = (
        P(blk, tp),
        P(blk, tp),
        P(blk, tp),
        P(),
        P(None, tp),
        P(None, tp),
        P(None, tp),
        P(blk, tp),
        P(blk, tp),
        P(),
        P(None, blk),
        P(tp, None),
        P(blk, tp),
        P(None, tp),
    )
    return jax.shard_map(
        on_device,
        mesh=split_mesh,
        in_specs=placed,
        out_specs=(P(blk, tp), P(None, tp)),
        check_vma=False,
    )
```

```python
import functools

import jax
import jax.numpy as jnp
from jax import lax
from jax.experimental import pallas as pl
from jax.experimental.pallas import tpu as pltpu
from jax.sharding import Mesh
from jax.sharding import PartitionSpec as P

HEAD_DIM = 128
PAGE = 128
DEC = 12
KEY_BLOCK = 512
LONGEST_DOC = 10240

NEGATIVE = -1e30

BLK_AXES = ("z", "y", "xh")
TP_AXES = ("xl", "c")


def prefill_kernel(
    first_ref, last_ref, start_ref, kind_ref, bdoc_ref, q_ref, kv_ref, kdoc_ref, qdoc_ref, m_in, l_in, acc_in,
    m_ref, l_ref, acc_ref, *, group, factor, piece, pieces,
):
    step = pl.program_id(0)
    block = (first_ref[0] // pieces) * pieces + piece + pieces * step
    active = (block >= first_ref[0]) & (block <= last_ref[0])
    clamped = jnp.minimum(jnp.maximum(block, first_ref[0]), last_ref[0])
    kind = kind_ref[clamped]

    @pl.when(step == 0)
    def _():
        m_ref[...] = m_in[...]
        l_ref[...] = l_in[...]
        acc_ref[...] = acc_in[...]

    def accumulate(mode):
        kv = kv_ref[...]
        keys = kv[:, :HEAD_DIM]
        values = kv[:, HEAD_DIM:]
        rows = q_ref.shape[0]
        scores = lax.dot_general(
            q_ref[...], keys, (((1,), (1,)), ((), ())), preferred_element_type=jnp.float32
        ) * factor
        old_top = m_ref[...]
        if mode == 0:
            query_where = start_ref[0] + lax.broadcasted_iota(jnp.int32, (rows, 1), 0) // group
            key_where = block * KEY_BLOCK + lax.broadcasted_iota(jnp.int32, (1, KEY_BLOCK), 1)
            visible = (qdoc_ref[...] == kdoc_ref[...]) & (key_where <= query_where)
            scores = jnp.where(visible, scores, NEGATIVE)
            new_top = jnp.maximum(old_top, jnp.max(scores, axis=1, keepdims=True))
            weights = jnp.where(visible, jnp.exp(scores - new_top), 0.0).astype(jnp.bfloat16)
        else:
            new_top = jnp.maximum(old_top, jnp.max(scores, axis=1, keepdims=True))
            weights = jnp.exp(scores - new_top).astype(jnp.bfloat16)
        rescale = jnp.exp(old_top - new_top)
        new_total = l_ref[...] * rescale + jnp.sum(weights.astype(jnp.float32), axis=1, keepdims=True)
        new_vector = acc_ref[...] * rescale + jnp.dot(
            weights, values, preferred_element_type=jnp.float32
        )
        if mode == 2:
            seen = qdoc_ref[...] == bdoc_ref[clamped]
            new_top = jnp.where(seen, new_top, old_top)
            new_total = jnp.where(seen, new_total, l_ref[...])
            new_vector = jnp.where(seen, new_vector, acc_ref[...])
        l_ref[...] = new_total
        acc_ref[...] = new_vector
        m_ref[...] = new_top

    for mode in (0, 1, 2):

        @pl.when(active & (kind == mode))
        def _():
            accumulate(mode)


def prefill_attention(q_rows, parts, docs, query_docs, query_start, first_block, last_block, group, factor):
    rows = q_rows.shape[0]
    token_count = docs.shape[0]
    pieces = len(parts)
    span = min(
        token_count // KEY_BLOCK,
        (LONGEST_DOC - 1 + rows // group - 1) // KEY_BLOCK + 2,
    )
    steps = (span - 1 + pieces - 1) // pieces + 1
    row_docs = jnp.repeat(query_docs, group)[:, None]
    block_ids = jnp.arange(token_count // KEY_BLOCK, dtype=jnp.int32)
    block_docs = docs[::KEY_BLOCK]
    one_doc = (block_docs == docs[KEY_BLOCK - 1 :: KEY_BLOCK]) & (
        (block_ids + 1) * KEY_BLOCK <= query_start
    )
    whole = one_doc & (block_docs == query_docs[0]) & (block_docs == query_docs[-1])
    kinds = jnp.where(whole, 1, jnp.where(one_doc, 2, 0)).astype(jnp.int32)
    key_docs = docs.reshape(1, token_count)

    def visited(i, first, last, piece):
        block = (first[0] // pieces) * pieces + piece + pieces * i
        return jnp.minimum(jnp.maximum(block, first[0]), last[0])


    def fixed(i, first, last, start, kind, bdoc):
        return (0, 0)

    state_specs = [
        pl.BlockSpec((rows, 1), fixed),
        pl.BlockSpec((rows, 1), fixed),
        pl.BlockSpec((rows, HEAD_DIM), fixed),
    ]
    def grid_spec(piece):
        return pltpu.PrefetchScalarGridSpec(
            num_scalar_prefetch=5,
            grid=(steps,),
            in_specs=[
                pl.BlockSpec((rows, HEAD_DIM), fixed),
                pl.BlockSpec(
                    (KEY_BLOCK, parts[0].shape[1]),
                    lambda i, first, last, start, kind, bdoc: (visited(i, first, last, piece) // pieces, 0),
                ),
                pl.BlockSpec(
                    (1, KEY_BLOCK),
                    lambda i, first, last, start, kind, bdoc: (0, visited(i, first, last, piece)),
                ),
                pl.BlockSpec((rows, 1), fixed),
            ]
            + state_specs,
            out_specs=state_specs,
        )

    scalars = (
        jnp.reshape(first_block, (1,)).astype(jnp.int32),
        jnp.reshape(last_block, (1,)).astype(jnp.int32),
        jnp.reshape(query_start, (1,)).astype(jnp.int32),
        kinds,
        block_docs.astype(jnp.int32),
    )
    state = (
        jnp.full((rows, 1), NEGATIVE, jnp.float32),
        jnp.zeros((rows, 1), jnp.float32),
        jnp.zeros((rows, HEAD_DIM), jnp.float32),
    )
    for piece, kv_part in enumerate(parts):
        state = pl.pallas_call(
            functools.partial(prefill_kernel, group=group, factor=factor, piece=piece, pieces=pieces),
            grid_spec=grid_spec(piece),
            out_shape=[jax.ShapeDtypeStruct(part.shape, jnp.float32) for part in state],
            compiler_params=pltpu.CompilerParams(dimension_semantics=("arbitrary",)),
        )(*scalars, q_rows, kv_part, key_docs, row_docs, *state)
    final_top, final_total, final_vector = state
    return (final_vector / final_total).astype(jnp.bfloat16)


def merge_partials(packed, axis):
    pieces = lax.all_gather(packed, axis, axis=0, tiled=False)
    tops = pieces[..., HEAD_DIM + 1]
    top = jnp.max(tops, axis=0)
    scale = jnp.exp(tops - top[None])
    summed = jnp.sum(pieces[..., : HEAD_DIM + 1] * scale[..., None], axis=0)
    return jnp.concatenate([summed, top[..., None]], axis=-1)


def prefetch_weights(w_out):
    half = w_out.shape[1] // 2
    first_x = lax.axis_index("xl") == 0
    keep = jnp.where(first_x, w_out[:, :half], w_out[:, half:])
    send = jnp.where(first_x, w_out[:, half:], w_out[:, :half])
    return keep, send


def project_tp(joined, w_keep, w_partner):
    partner_rows = lax.ppermute(joined, "xl", [(0, 1), (1, 0)])
    partial = jnp.dot(joined, w_keep, preferred_element_type=jnp.float32)
    partial = partial + jnp.dot(partner_rows, w_partner, preferred_element_type=jnp.float32)
    quarter = partial.shape[1] // 2
    first_core = lax.axis_index("c") == 0
    send = jnp.where(first_core, partial[:, quarter:], partial[:, :quarter])
    keep = jnp.where(first_core, partial[:, :quarter], partial[:, quarter:])
    return keep + lax.ppermute(send, "c", [(0, 1), (1, 0)])


def on_device(
    q_pre,
    k_pre,
    v_pre,
    docs,
    q_dec,
    k_dec,
    v_dec,
    k_cache,
    v_cache,
    lengths,
    page_map,
    w_out,
    resid_pre,
    resid_dec,
):
    query_rows = q_pre.shape[0]
    local_heads = q_pre.shape[1] // HEAD_DIM
    local_kv = k_pre.shape[1] // HEAD_DIM
    group_size = local_heads // local_kv
    factor = HEAD_DIM ** (-0.5)
    blk_index = (
        lax.axis_index("z") * (lax.axis_size("y") * lax.axis_size("xh"))
        + lax.axis_index("y") * lax.axis_size("xh")
        + lax.axis_index("xh")
    )
    query_start = blk_index * query_rows
    query_docs = lax.dynamic_slice_in_dim(docs, query_start, query_rows, 0)

    w_keep, w_send = prefetch_weights(w_out)

    joined_kv = jnp.concatenate([k_pre, v_pre], axis=1)
    for axis in ("xh", "y"):
        joined_kv = lax.all_gather(joined_kv, axis, axis=0, tiled=True)
    group_blocks = joined_kv.shape[0] // KEY_BLOCK
    parts = [
        lax.all_gather(joined_kv[p * KEY_BLOCK : (p + 1) * KEY_BLOCK], "z", axis=0, tiled=True)
        for p in range(group_blocks)
    ]

    doc_start = jnp.sum((docs < query_docs[0]).astype(jnp.int32))
    first_block = doc_start // KEY_BLOCK
    last_block = (query_start + query_rows - 1) // KEY_BLOCK

    attn_rows = prefill_attention(
        q_pre.reshape(query_rows * local_heads, HEAD_DIM),
        parts,
        docs,
        query_docs,
        query_start,
        first_block,
        last_block,
        group_size,
        factor,
    )
    attn_pre = attn_rows.reshape(query_rows, local_heads * HEAD_DIM)

    page_count = page_map.shape[1]
    page_owner = page_map[0]
    page_index = page_map[1]
    requests = jnp.arange(DEC, dtype=jnp.int32)
    belongs = page_owner[:, None] == requests[None, :]
    query_pages = jnp.dot(belongs.astype(jnp.bfloat16), q_dec, preferred_element_type=jnp.float32)
    query_pages = query_pages.astype(jnp.bfloat16).reshape(
        page_count, local_kv, group_size, HEAD_DIM
    )
    page_keys = k_cache.reshape(page_count, PAGE, local_kv, HEAD_DIM)
    page_values = v_cache.reshape(page_count, PAGE, local_kv, HEAD_DIM)
    safe_owner = jnp.minimum(page_owner, DEC - 1)
    positions = page_index[:, None] * PAGE + jnp.arange(PAGE, dtype=jnp.int32)[None, :]
    live_rows = (page_owner[:, None] < DEC) & (positions < lengths[safe_owner][:, None])
    live_mask = live_rows[:, None, None, :]
    page_scores = (
        jnp.einsum("pkgd,ptkd->pkgt", query_pages, page_keys, preferred_element_type=jnp.float32)
        * factor
    )
    page_scores = jnp.where(live_mask, page_scores, NEGATIVE)
    page_top = jnp.max(page_scores, axis=-1)
    request_top = jnp.max(jnp.where(belongs[:, :, None, None], page_top[:, None], NEGATIVE), axis=0)
    shared_top = request_top[safe_owner]
    page_weights = jnp.where(live_mask, jnp.exp(page_scores - shared_top[..., None]), 0.0).astype(
        jnp.bfloat16
    )
    page_weights = lax.optimization_barrier(page_weights)
    page_total = jnp.sum(page_weights.astype(jnp.float32), axis=-1)
    page_vector = jnp.einsum(
        "pkgt,ptkd->pkgd", page_weights, page_values, preferred_element_type=jnp.float32
    )
    membership = belongs.astype(jnp.float32)
    request_total = jnp.einsum(
        "pr,pkg->rkg", membership, page_total, precision=lax.Precision.HIGHEST
    )
    request_vector = jnp.einsum(
        "pr,pkgd->rkgd", membership, page_vector, precision=lax.Precision.HIGHEST
    )
    packed = jnp.concatenate(
        [request_vector, request_total[..., None], request_top[..., None]], axis=-1
    )
    for axis in ("xh", "y", "z"):
        packed = merge_partials(packed, axis)
    packed, w_send = lax.optimization_barrier((packed, w_send))
    w_partner = lax.ppermute(w_send, "xl", [(0, 1), (1, 0)])
    merged_vector = packed[..., :HEAD_DIM]
    merged_total = packed[..., HEAD_DIM]
    merged_top = packed[..., HEAD_DIM + 1]

    dec_queries = q_dec.reshape(DEC, local_kv, group_size, HEAD_DIM)
    own_scores = (
        jnp.einsum(
            "rkgd,rkd->rkg",
            dec_queries,
            k_dec.reshape(DEC, local_kv, HEAD_DIM),
            preferred_element_type=jnp.float32,
        )
        * factor
    )
    joint_top = jnp.maximum(merged_top, own_scores)
    own_weight = jnp.exp(own_scores - joint_top).astype(jnp.bfloat16)
    own_weight = lax.optimization_barrier(own_weight).astype(jnp.float32)
    carried_scale = jnp.exp(merged_top - joint_top)
    numerator = merged_vector * carried_scale[..., None] + own_weight[..., None] * v_dec.reshape(
        DEC, local_kv, 1, HEAD_DIM
    ).astype(jnp.float32)
    denominator = merged_total * carried_scale + own_weight
    attn_dec = (
        (numerator / denominator[..., None])
        .reshape(DEC, local_heads * HEAD_DIM)
        .astype(jnp.bfloat16)
    )
    joined = jnp.concatenate([attn_pre, attn_dec], axis=0)
    summed = project_tp(joined, w_keep, w_partner)
    out_pre = resid_pre.astype(jnp.float32) + summed[:query_rows]
    out_dec = resid_dec.astype(jnp.float32) + summed[query_rows:]
    return (out_pre, out_dec)


def solution(mesh):
    blk_size, tp_size = mesh.devices.shape
    split_mesh = Mesh(
        mesh.devices.reshape(8, 4, blk_size // 32, 2, tp_size // 2),
        BLK_AXES + TP_AXES,
    )
    blk = BLK_AXES
    tp = TP_AXES
    placed = (
        P(blk, tp),
        P(blk, tp),
        P(blk, tp),
        P(),
        P(None, tp),
        P(None, tp),
        P(None, tp),
        P(blk, tp),
        P(blk, tp),
        P(),
        P(None, blk),
        P(tp, None),
        P(blk, tp),
        P(None, tp),
    )
    return jax.shard_map(
        on_device,
        mesh=split_mesh,
        in_specs=placed,
        out_specs=(P(blk, tp), P(None, tp)),
        check_vma=False,
    )
```

```python
import functools

import jax
import jax.numpy as jnp
from jax import lax
from jax.experimental import pallas as pl
from jax.experimental.pallas import tpu as pltpu
from jax.sharding import Mesh
from jax.sharding import PartitionSpec as P

HEAD_DIM = 128
PAGE = 128
DEC = 12
KEY_BLOCK = 512
LONGEST_DOC = 10240

NEGATIVE = -1e30

BLK_AXES = ("z", "y", "xh")
TP_AXES = ("xl", "c")


def prefill_kernel(
    first_ref, last_ref, start_ref, kind_ref, bdoc_ref, q_ref, kv_ref, kdoc_ref, qdoc_ref, m_in, l_in, acc_in,
    m_ref, l_ref, acc_ref, *, group, factor, half, half_blocks,
):
    step = pl.program_id(0)
    block = first_ref[0] + step
    active = (block <= last_ref[0]) & ((block // half_blocks) % 2 == half)
    clamped = jnp.minimum(block, last_ref[0])
    kind = kind_ref[clamped]

    @pl.when(step == 0)
    def _():
        m_ref[...] = m_in[...]
        l_ref[...] = l_in[...]
        acc_ref[...] = acc_in[...]

    def accumulate(mode):
        kv = kv_ref[...]
        keys = kv[:, :HEAD_DIM]
        values = kv[:, HEAD_DIM:]
        rows = q_ref.shape[0]
        scores = lax.dot_general(
            q_ref[...], keys, (((1,), (1,)), ((), ())), preferred_element_type=jnp.float32
        ) * factor
        old_top = m_ref[...]
        if mode == 0:
            query_where = start_ref[0] + lax.broadcasted_iota(jnp.int32, (rows, 1), 0) // group
            key_where = block * KEY_BLOCK + lax.broadcasted_iota(jnp.int32, (1, KEY_BLOCK), 1)
            visible = (qdoc_ref[...] == kdoc_ref[...]) & (key_where <= query_where)
            scores = jnp.where(visible, scores, NEGATIVE)
            new_top = jnp.maximum(old_top, jnp.max(scores, axis=1, keepdims=True))
            weights = jnp.where(visible, jnp.exp(scores - new_top), 0.0).astype(jnp.bfloat16)
        else:
            new_top = jnp.maximum(old_top, jnp.max(scores, axis=1, keepdims=True))
            weights = jnp.exp(scores - new_top).astype(jnp.bfloat16)
        rescale = jnp.exp(old_top - new_top)
        ones = jnp.ones((KEY_BLOCK, HEAD_DIM), jnp.bfloat16)
        row_sums = jnp.dot(weights, ones, preferred_element_type=jnp.float32)[:, :1]
        new_total = l_ref[...] * rescale + row_sums
        new_vector = acc_ref[...] * rescale + jnp.dot(
            weights, values, preferred_element_type=jnp.float32
        )
        if mode == 2:
            seen = qdoc_ref[...] == bdoc_ref[clamped]
            new_top = jnp.where(seen, new_top, old_top)
            new_total = jnp.where(seen, new_total, l_ref[...])
            new_vector = jnp.where(seen, new_vector, acc_ref[...])
        l_ref[...] = new_total
        acc_ref[...] = new_vector
        m_ref[...] = new_top

    for mode in (0, 1, 2):

        @pl.when(active & (kind == mode))
        def _():
            accumulate(mode)


def prefill_attention(q_rows, halves, docs, query_docs, query_start, first_block, last_block, group, factor):
    rows = q_rows.shape[0]
    token_count = docs.shape[0]
    group_blocks = 2 * halves[0].shape[0] // (KEY_BLOCK * lax.axis_size("z"))
    half_blocks = group_blocks // 2
    steps = min(
        token_count // KEY_BLOCK,
        (LONGEST_DOC - 1 + rows // group - 1) // KEY_BLOCK + 2,
    )
    row_docs = jnp.repeat(query_docs, group)[:, None]
    block_ids = jnp.arange(token_count // KEY_BLOCK, dtype=jnp.int32)
    block_docs = docs[::KEY_BLOCK]
    one_doc = (block_docs == docs[KEY_BLOCK - 1 :: KEY_BLOCK]) & (
        (block_ids + 1) * KEY_BLOCK <= query_start
    )
    whole = one_doc & (block_docs == query_docs[0]) & (block_docs == query_docs[-1])
    kinds = jnp.where(whole, 1, jnp.where(one_doc, 2, 0)).astype(jnp.int32)
    key_docs = docs.reshape(1, token_count)

    def kv_map(i, first, last, start, kind, bdoc):
        block = jnp.minimum(first[0] + i, last[0])
        return ((block // group_blocks) * half_blocks + block % half_blocks, 0)

    def doc_map(i, first, last, start, kind, bdoc):
        return (0, jnp.minimum(first[0] + i, last[0]))

    def fixed(i, first, last, start, kind, bdoc):
        return (0, 0)

    state_specs = [
        pl.BlockSpec((rows, 1), fixed),
        pl.BlockSpec((rows, 1), fixed),
        pl.BlockSpec((rows, HEAD_DIM), fixed),
    ]
    grid_spec = pltpu.PrefetchScalarGridSpec(
        num_scalar_prefetch=5,
        grid=(steps,),
        in_specs=[
            pl.BlockSpec((rows, HEAD_DIM), fixed),
            pl.BlockSpec((KEY_BLOCK, halves[0].shape[1]), kv_map),
            pl.BlockSpec((1, KEY_BLOCK), doc_map),
            pl.BlockSpec((rows, 1), fixed),
        ]
        + state_specs,
        out_specs=state_specs,
    )
    scalars = (
        jnp.reshape(first_block, (1,)).astype(jnp.int32),
        jnp.reshape(last_block, (1,)).astype(jnp.int32),
        jnp.reshape(query_start, (1,)).astype(jnp.int32),
        kinds,
        block_docs.astype(jnp.int32),
    )
    state = (
        jnp.full((rows, 1), NEGATIVE, jnp.float32),
        jnp.zeros((rows, 1), jnp.float32),
        jnp.zeros((rows, HEAD_DIM), jnp.float32),
    )
    for half, kv_half in enumerate(halves):
        state = pl.pallas_call(
            functools.partial(
                prefill_kernel, group=group, factor=factor, half=half, half_blocks=half_blocks
            ),
            grid_spec=grid_spec,
            out_shape=[jax.ShapeDtypeStruct(part.shape, jnp.float32) for part in state],
            compiler_params=pltpu.CompilerParams(dimension_semantics=("arbitrary",)),
        )(*scalars, q_rows, kv_half, key_docs, row_docs, *state)
    final_top, final_total, final_vector = state
    return (final_vector / final_total).astype(jnp.bfloat16)


def merge_partials(packed, axis):
    pieces = lax.all_gather(packed, axis, axis=0, tiled=False)
    tops = pieces[..., HEAD_DIM + 1]
    top = jnp.max(tops, axis=0)
    scale = jnp.exp(tops - top[None])
    summed = jnp.sum(pieces[..., : HEAD_DIM + 1] * scale[..., None], axis=0)
    return jnp.concatenate([summed, top[..., None]], axis=-1)


def prefetch_weights(w_out):
    half = w_out.shape[1] // 2
    first_x = lax.axis_index("xl") == 0
    keep = jnp.where(first_x, w_out[:, :half], w_out[:, half:])
    send = jnp.where(first_x, w_out[:, half:], w_out[:, :half])
    return keep, send


def project_tp(joined, w_keep, w_partner):
    partner_rows = lax.ppermute(joined, "xl", [(0, 1), (1, 0)])
    partial = jnp.dot(joined, w_keep, preferred_element_type=jnp.float32)
    partial = partial + jnp.dot(partner_rows, w_partner, preferred_element_type=jnp.float32)
    quarter = partial.shape[1] // 2
    first_core = lax.axis_index("c") == 0
    send = jnp.where(first_core, partial[:, quarter:], partial[:, :quarter])
    keep = jnp.where(first_core, partial[:, :quarter], partial[:, quarter:])
    return keep + lax.ppermute(send, "c", [(0, 1), (1, 0)])


def on_device(
    q_pre,
    k_pre,
    v_pre,
    docs,
    q_dec,
    k_dec,
    v_dec,
    k_cache,
    v_cache,
    lengths,
    page_map,
    w_out,
    resid_pre,
    resid_dec,
):
    query_rows = q_pre.shape[0]
    local_heads = q_pre.shape[1] // HEAD_DIM
    local_kv = k_pre.shape[1] // HEAD_DIM
    group_size = local_heads // local_kv
    factor = HEAD_DIM ** (-0.5)
    blk_index = (
        lax.axis_index("z") * (lax.axis_size("y") * lax.axis_size("xh"))
        + lax.axis_index("y") * lax.axis_size("xh")
        + lax.axis_index("xh")
    )
    query_start = blk_index * query_rows
    query_docs = lax.dynamic_slice_in_dim(docs, query_start, query_rows, 0)

    w_keep, w_send = prefetch_weights(w_out)

    joined_kv = jnp.concatenate([k_pre, v_pre], axis=1)
    for axis in ("xh", "y"):
        joined_kv = lax.all_gather(joined_kv, axis, axis=0, tiled=True)
    split = joined_kv.shape[0] // 2
    halves = [
        lax.all_gather(joined_kv[:split], "z", axis=0, tiled=True),
        lax.all_gather(joined_kv[split:], "z", axis=0, tiled=True),
    ]

    doc_start = jnp.sum((docs < query_docs[0]).astype(jnp.int32))
    first_block = doc_start // KEY_BLOCK
    last_block = (query_start + query_rows - 1) // KEY_BLOCK

    attn_rows = prefill_attention(
        q_pre.reshape(query_rows * local_heads, HEAD_DIM),
        halves,
        docs,
        query_docs,
        query_start,
        first_block,
        last_block,
        group_size,
        factor,
    )
    attn_pre = attn_rows.reshape(query_rows, local_heads * HEAD_DIM)

    page_count = page_map.shape[1]
    page_owner = page_map[0]
    page_index = page_map[1]
    requests = jnp.arange(DEC, dtype=jnp.int32)
    belongs = page_owner[:, None] == requests[None, :]
    query_pages = jnp.dot(belongs.astype(jnp.bfloat16), q_dec, preferred_element_type=jnp.float32)
    query_pages = query_pages.astype(jnp.bfloat16).reshape(
        page_count, local_kv, group_size, HEAD_DIM
    )
    page_keys = k_cache.reshape(page_count, PAGE, local_kv, HEAD_DIM)
    page_values = v_cache.reshape(page_count, PAGE, local_kv, HEAD_DIM)
    safe_owner = jnp.minimum(page_owner, DEC - 1)
    positions = page_index[:, None] * PAGE + jnp.arange(PAGE, dtype=jnp.int32)[None, :]
    live_rows = (page_owner[:, None] < DEC) & (positions < lengths[safe_owner][:, None])
    live_mask = live_rows[:, None, None, :]
    page_scores = (
        jnp.einsum("pkgd,ptkd->pkgt", query_pages, page_keys, preferred_element_type=jnp.float32)
        * factor
    )
    page_scores = jnp.where(live_mask, page_scores, NEGATIVE)
    page_top = jnp.max(page_scores, axis=-1)
    request_top = jnp.max(jnp.where(belongs[:, :, None, None], page_top[:, None], NEGATIVE), axis=0)
    shared_top = request_top[safe_owner]
    page_weights = jnp.where(live_mask, jnp.exp(page_scores - shared_top[..., None]), 0.0).astype(
        jnp.bfloat16
    )
    page_weights = lax.optimization_barrier(page_weights)
    page_total = jnp.sum(page_weights.astype(jnp.float32), axis=-1)
    page_vector = jnp.einsum(
        "pkgt,ptkd->pkgd", page_weights, page_values, preferred_element_type=jnp.float32
    )
    membership = belongs.astype(jnp.float32)
    request_total = jnp.einsum(
        "pr,pkg->rkg", membership, page_total, precision=lax.Precision.HIGHEST
    )
    request_vector = jnp.einsum(
        "pr,pkgd->rkgd", membership, page_vector, precision=lax.Precision.HIGHEST
    )
    packed = jnp.concatenate(
        [request_vector, request_total[..., None], request_top[..., None]], axis=-1
    )
    for axis in ("xh", "y", "z"):
        packed = merge_partials(packed, axis)
    packed, w_send = lax.optimization_barrier((packed, w_send))
    w_partner = lax.ppermute(w_send, "xl", [(0, 1), (1, 0)])
    merged_vector = packed[..., :HEAD_DIM]
    merged_total = packed[..., HEAD_DIM]
    merged_top = packed[..., HEAD_DIM + 1]

    dec_queries = q_dec.reshape(DEC, local_kv, group_size, HEAD_DIM)
    own_scores = (
        jnp.einsum(
            "rkgd,rkd->rkg",
            dec_queries,
            k_dec.reshape(DEC, local_kv, HEAD_DIM),
            preferred_element_type=jnp.float32,
        )
        * factor
    )
    joint_top = jnp.maximum(merged_top, own_scores)
    own_weight = jnp.exp(own_scores - joint_top).astype(jnp.bfloat16)
    own_weight = lax.optimization_barrier(own_weight).astype(jnp.float32)
    carried_scale = jnp.exp(merged_top - joint_top)
    numerator = merged_vector * carried_scale[..., None] + own_weight[..., None] * v_dec.reshape(
        DEC, local_kv, 1, HEAD_DIM
    ).astype(jnp.float32)
    denominator = merged_total * carried_scale + own_weight
    attn_dec = (
        (numerator / denominator[..., None])
        .reshape(DEC, local_heads * HEAD_DIM)
        .astype(jnp.bfloat16)
    )
    joined = jnp.concatenate([attn_pre, attn_dec], axis=0)
    summed = project_tp(joined, w_keep, w_partner)
    out_pre = resid_pre.astype(jnp.float32) + summed[:query_rows]
    out_dec = resid_dec.astype(jnp.float32) + summed[query_rows:]
    return (out_pre, out_dec)


def solution(mesh):
    blk_size, tp_size = mesh.devices.shape
    split_mesh = Mesh(
        mesh.devices.reshape(8, 4, blk_size // 32, 2, tp_size // 2),
        BLK_AXES + TP_AXES,
    )
    blk = BLK_AXES
    tp = TP_AXES
    placed = (
        P(blk, tp),
        P(blk, tp),
        P(blk, tp),
        P(),
        P(None, tp),
        P(None, tp),
        P(None, tp),
        P(blk, tp),
        P(blk, tp),
        P(),
        P(None, blk),
        P(tp, None),
        P(blk, tp),
        P(None, tp),
    )
    return jax.shard_map(
        on_device,
        mesh=split_mesh,
        in_specs=placed,
        out_specs=(P(blk, tp), P(None, tp)),
        check_vma=False,
    )
```

```python
import functools

import jax
import jax.numpy as jnp
from jax import lax
from jax.experimental import pallas as pl
from jax.experimental.pallas import tpu as pltpu
from jax.sharding import Mesh
from jax.sharding import PartitionSpec as P

HEAD_DIM = 128
PAGE = 128
DEC = 12
KEY_BLOCK = 1024
LONGEST_DOC = 10240

NEGATIVE = -1e30

BLK_AXES = ("z", "y", "xh")
TP_AXES = ("xl", "c")


def prefill_kernel(
    first_ref, last_ref, start_ref, kind_ref, bdoc_ref, q_ref, kv_ref, kdoc_ref, qdoc_ref, m_in, l_in, acc_in,
    m_ref, l_ref, acc_ref, *, group, factor, half, half_blocks,
):
    step = pl.program_id(0)
    block = first_ref[0] + step
    active = (block <= last_ref[0]) & ((block // half_blocks) % 2 == half)
    clamped = jnp.minimum(block, last_ref[0])
    kind = kind_ref[clamped]

    @pl.when(step == 0)
    def _():
        m_ref[...] = m_in[...]
        l_ref[...] = l_in[...]
        acc_ref[...] = acc_in[...]

    def accumulate(mode):
        kv = kv_ref[...]
        keys = kv[:, :HEAD_DIM]
        values = kv[:, HEAD_DIM:]
        rows = q_ref.shape[0]
        scores = lax.dot_general(
            q_ref[...], keys, (((1,), (1,)), ((), ())), preferred_element_type=jnp.float32
        ) * factor
        old_top = m_ref[...]
        if mode == 0:
            query_where = start_ref[0] + lax.broadcasted_iota(jnp.int32, (rows, 1), 0) // group
            key_where = block * KEY_BLOCK + lax.broadcasted_iota(jnp.int32, (1, KEY_BLOCK), 1)
            visible = (qdoc_ref[...] == kdoc_ref[...]) & (key_where <= query_where)
            scores = jnp.where(visible, scores, NEGATIVE)
            new_top = jnp.maximum(old_top, jnp.max(scores, axis=1, keepdims=True))
            weights = jnp.where(visible, jnp.exp(scores - new_top), 0.0).astype(jnp.bfloat16)
        else:
            new_top = jnp.maximum(old_top, jnp.max(scores, axis=1, keepdims=True))
            weights = jnp.exp(scores - new_top).astype(jnp.bfloat16)
        rescale = jnp.exp(old_top - new_top)
        ones = jnp.ones((KEY_BLOCK, HEAD_DIM), jnp.bfloat16)
        row_sums = jnp.dot(weights, ones, preferred_element_type=jnp.float32)[:, :1]
        new_total = l_ref[...] * rescale + row_sums
        new_vector = acc_ref[...] * rescale + jnp.dot(
            weights, values, preferred_element_type=jnp.float32
        )
        if mode == 2:
            seen = qdoc_ref[...] == bdoc_ref[clamped]
            new_top = jnp.where(seen, new_top, old_top)
            new_total = jnp.where(seen, new_total, l_ref[...])
            new_vector = jnp.where(seen, new_vector, acc_ref[...])
        l_ref[...] = new_total
        acc_ref[...] = new_vector
        m_ref[...] = new_top

    for mode in (0, 1, 2):

        @pl.when(active & (kind == mode))
        def _():
            accumulate(mode)


def prefill_attention(q_rows, halves, docs, query_docs, query_start, first_block, last_block, group, factor):
    rows = q_rows.shape[0]
    token_count = docs.shape[0]
    group_blocks = 2 * halves[0].shape[0] // (KEY_BLOCK * lax.axis_size("z"))
    half_blocks = group_blocks // 2
    steps = min(
        token_count // KEY_BLOCK,
        (LONGEST_DOC - 1 + rows // group - 1) // KEY_BLOCK + 2,
    )
    row_docs = jnp.repeat(query_docs, group)[:, None]
    block_ids = jnp.arange(token_count // KEY_BLOCK, dtype=jnp.int32)
    block_docs = docs[::KEY_BLOCK]
    one_doc = (block_docs == docs[KEY_BLOCK - 1 :: KEY_BLOCK]) & (
        (block_ids + 1) * KEY_BLOCK <= query_start
    )
    whole = one_doc & (block_docs == query_docs[0]) & (block_docs == query_docs[-1])
    kinds = jnp.where(whole, 1, jnp.where(one_doc, 2, 0)).astype(jnp.int32)
    key_docs = docs.reshape(1, token_count)

    def kv_map(i, first, last, start, kind, bdoc):
        block = jnp.minimum(first[0] + i, last[0])
        return ((block // group_blocks) * half_blocks + block % half_blocks, 0)

    def doc_map(i, first, last, start, kind, bdoc):
        return (0, jnp.minimum(first[0] + i, last[0]))

    def fixed(i, first, last, start, kind, bdoc):
        return (0, 0)

    state_specs = [
        pl.BlockSpec((rows, 1), fixed),
        pl.BlockSpec((rows, 1), fixed),
        pl.BlockSpec((rows, HEAD_DIM), fixed),
    ]
    grid_spec = pltpu.PrefetchScalarGridSpec(
        num_scalar_prefetch=5,
        grid=(steps,),
        in_specs=[
            pl.BlockSpec((rows, HEAD_DIM), fixed),
            pl.BlockSpec((KEY_BLOCK, halves[0].shape[1]), kv_map),
            pl.BlockSpec((1, KEY_BLOCK), doc_map),
            pl.BlockSpec((rows, 1), fixed),
        ]
        + state_specs,
        out_specs=state_specs,
    )
    scalars = (
        jnp.reshape(first_block, (1,)).astype(jnp.int32),
        jnp.reshape(last_block, (1,)).astype(jnp.int32),
        jnp.reshape(query_start, (1,)).astype(jnp.int32),
        kinds,
        block_docs.astype(jnp.int32),
    )
    state = (
        jnp.full((rows, 1), NEGATIVE, jnp.float32),
        jnp.zeros((rows, 1), jnp.float32),
        jnp.zeros((rows, HEAD_DIM), jnp.float32),
    )
    for half, kv_half in enumerate(halves):
        state = pl.pallas_call(
            functools.partial(
                prefill_kernel, group=group, factor=factor, half=half, half_blocks=half_blocks
            ),
            grid_spec=grid_spec,
            out_shape=[jax.ShapeDtypeStruct(part.shape, jnp.float32) for part in state],
            compiler_params=pltpu.CompilerParams(dimension_semantics=("arbitrary",)),
        )(*scalars, q_rows, kv_half, key_docs, row_docs, *state)
    final_top, final_total, final_vector = state
    return (final_vector / final_total).astype(jnp.bfloat16)


def merge_partials(packed, axis):
    pieces = lax.all_gather(packed, axis, axis=0, tiled=False)
    tops = pieces[..., HEAD_DIM + 1]
    top = jnp.max(tops, axis=0)
    scale = jnp.exp(tops - top[None])
    summed = jnp.sum(pieces[..., : HEAD_DIM + 1] * scale[..., None], axis=0)
    return jnp.concatenate([summed, top[..., None]], axis=-1)


def prefetch_weights(w_out):
    half = w_out.shape[1] // 2
    first_x = lax.axis_index("xl") == 0
    keep = jnp.where(first_x, w_out[:, :half], w_out[:, half:])
    send = jnp.where(first_x, w_out[:, half:], w_out[:, :half])
    return keep, send


def project_tp(joined, w_keep, w_partner):
    partner_rows = lax.ppermute(joined, "xl", [(0, 1), (1, 0)])
    partial = jnp.dot(joined, w_keep, preferred_element_type=jnp.float32)
    partial = partial + jnp.dot(partner_rows, w_partner, preferred_element_type=jnp.float32)
    quarter = partial.shape[1] // 2
    first_core = lax.axis_index("c") == 0
    send = jnp.where(first_core, partial[:, quarter:], partial[:, :quarter])
    keep = jnp.where(first_core, partial[:, :quarter], partial[:, quarter:])
    return keep + lax.ppermute(send, "c", [(0, 1), (1, 0)])


def on_device(
    q_pre,
    k_pre,
    v_pre,
    docs,
    q_dec,
    k_dec,
    v_dec,
    k_cache,
    v_cache,
    lengths,
    page_map,
    w_out,
    resid_pre,
    resid_dec,
):
    query_rows = q_pre.shape[0]
    local_heads = q_pre.shape[1] // HEAD_DIM
    local_kv = k_pre.shape[1] // HEAD_DIM
    group_size = local_heads // local_kv
    factor = HEAD_DIM ** (-0.5)
    blk_index = (
        lax.axis_index("z") * (lax.axis_size("y") * lax.axis_size("xh"))
        + lax.axis_index("y") * lax.axis_size("xh")
        + lax.axis_index("xh")
    )
    query_start = blk_index * query_rows
    query_docs = lax.dynamic_slice_in_dim(docs, query_start, query_rows, 0)

    w_keep, w_send = prefetch_weights(w_out)

    joined_kv = jnp.concatenate([k_pre, v_pre], axis=1)
    for axis in ("xh", "y"):
        joined_kv = lax.all_gather(joined_kv, axis, axis=0, tiled=True)
    split = joined_kv.shape[0] // 2
    halves = [
        lax.all_gather(joined_kv[:split], "z", axis=0, tiled=True),
        lax.all_gather(joined_kv[split:], "z", axis=0, tiled=True),
    ]

    doc_start = jnp.sum((docs < query_docs[0]).astype(jnp.int32))
    first_block = doc_start // KEY_BLOCK
    last_block = (query_start + query_rows - 1) // KEY_BLOCK

    attn_rows = prefill_attention(
        q_pre.reshape(query_rows * local_heads, HEAD_DIM),
        halves,
        docs,
        query_docs,
        query_start,
        first_block,
        last_block,
        group_size,
        factor,
    )
    attn_pre = attn_rows.reshape(query_rows, local_heads * HEAD_DIM)

    page_count = page_map.shape[1]
    page_owner = page_map[0]
    page_index = page_map[1]
    requests = jnp.arange(DEC, dtype=jnp.int32)
    belongs = page_owner[:, None] == requests[None, :]
    query_pages = jnp.dot(belongs.astype(jnp.bfloat16), q_dec, preferred_element_type=jnp.float32)
    query_pages = query_pages.astype(jnp.bfloat16).reshape(
        page_count, local_kv, group_size, HEAD_DIM
    )
    page_keys = k_cache.reshape(page_count, PAGE, local_kv, HEAD_DIM)
    page_values = v_cache.reshape(page_count, PAGE, local_kv, HEAD_DIM)
    safe_owner = jnp.minimum(page_owner, DEC - 1)
    positions = page_index[:, None] * PAGE + jnp.arange(PAGE, dtype=jnp.int32)[None, :]
    live_rows = (page_owner[:, None] < DEC) & (positions < lengths[safe_owner][:, None])
    live_mask = live_rows[:, None, None, :]
    page_scores = (
        jnp.einsum("pkgd,ptkd->pkgt", query_pages, page_keys, preferred_element_type=jnp.float32)
        * factor
    )
    page_scores = jnp.where(live_mask, page_scores, NEGATIVE)
    page_top = jnp.max(page_scores, axis=-1)
    request_top = jnp.max(jnp.where(belongs[:, :, None, None], page_top[:, None], NEGATIVE), axis=0)
    shared_top = request_top[safe_owner]
    page_weights = jnp.where(live_mask, jnp.exp(page_scores - shared_top[..., None]), 0.0).astype(
        jnp.bfloat16
    )
    page_weights = lax.optimization_barrier(page_weights)
    page_total = jnp.sum(page_weights.astype(jnp.float32), axis=-1)
    page_vector = jnp.einsum(
        "pkgt,ptkd->pkgd", page_weights, page_values, preferred_element_type=jnp.float32
    )
    membership = belongs.astype(jnp.float32)
    request_total = jnp.einsum(
        "pr,pkg->rkg", membership, page_total, precision=lax.Precision.HIGHEST
    )
    request_vector = jnp.einsum(
        "pr,pkgd->rkgd", membership, page_vector, precision=lax.Precision.HIGHEST
    )
    packed = jnp.concatenate(
        [request_vector, request_total[..., None], request_top[..., None]], axis=-1
    )
    for axis in ("xh", "y", "z"):
        packed = merge_partials(packed, axis)
    packed, w_send = lax.optimization_barrier((packed, w_send))
    w_partner = lax.ppermute(w_send, "xl", [(0, 1), (1, 0)])
    merged_vector = packed[..., :HEAD_DIM]
    merged_total = packed[..., HEAD_DIM]
    merged_top = packed[..., HEAD_DIM + 1]

    dec_queries = q_dec.reshape(DEC, local_kv, group_size, HEAD_DIM)
    own_scores = (
        jnp.einsum(
            "rkgd,rkd->rkg",
            dec_queries,
            k_dec.reshape(DEC, local_kv, HEAD_DIM),
            preferred_element_type=jnp.float32,
        )
        * factor
    )
    joint_top = jnp.maximum(merged_top, own_scores)
    own_weight = jnp.exp(own_scores - joint_top).astype(jnp.bfloat16)
    own_weight = lax.optimization_barrier(own_weight).astype(jnp.float32)
    carried_scale = jnp.exp(merged_top - joint_top)
    numerator = merged_vector * carried_scale[..., None] + own_weight[..., None] * v_dec.reshape(
        DEC, local_kv, 1, HEAD_DIM
    ).astype(jnp.float32)
    denominator = merged_total * carried_scale + own_weight
    attn_dec = (
        (numerator / denominator[..., None])
        .reshape(DEC, local_heads * HEAD_DIM)
        .astype(jnp.bfloat16)
    )
    joined = jnp.concatenate([attn_pre, attn_dec], axis=0)
    summed = project_tp(joined, w_keep, w_partner)
    out_pre = resid_pre.astype(jnp.float32) + summed[:query_rows]
    out_dec = resid_dec.astype(jnp.float32) + summed[query_rows:]
    return (out_pre, out_dec)


def solution(mesh):
    blk_size, tp_size = mesh.devices.shape
    split_mesh = Mesh(
        mesh.devices.reshape(8, 4, blk_size // 32, 2, tp_size // 2),
        BLK_AXES + TP_AXES,
    )
    blk = BLK_AXES
    tp = TP_AXES
    placed = (
        P(blk, tp),
        P(blk, tp),
        P(blk, tp),
        P(),
        P(None, tp),
        P(None, tp),
        P(None, tp),
        P(blk, tp),
        P(blk, tp),
        P(),
        P(None, blk),
        P(tp, None),
        P(blk, tp),
        P(None, tp),
    )
    return jax.shard_map(
        on_device,
        mesh=split_mesh,
        in_specs=placed,
        out_specs=(P(blk, tp), P(None, tp)),
        check_vma=False,
    )
```
